128 devices in a mesh: gz: 64 (over x, y_lo, z, core), xy: 2 (over y_hi).
Axes of the slice: x: 4, y: 4 (y_hi: 2, y_lo: 2; y = y_hi * 2 + y_lo), z: 4, core: 2. Of those that a mesh axis runs over, the one named last changes fastest.
Arguments:
- moments: bfloat16 [361, 512, 256], P(None, 'gz', 'xy'), may hold values from -4 to 4
- counts: int32 [512, 256], P('gz', 'xy'), may hold values from 0 to 7
- m2x: bfloat16 [1296, 361], replicated, may hold values from -0.3125 to 0.3125
- x2l: bfloat16 [361, 1296], replicated, may hold values from -0.0625 to 0.0625
- decay_rate: float32 [648], replicated, may hold values from 0.00048828125 to 0.05
- wave_x: float32 [648], replicated, may hold values from -3.140625 to 3.140625
- wave_y: float32 [648], replicated, may hold values from -3.140625 to 3.140625
- offsets: int32 [6, 2], replicated, may hold values from -2 to 2, as said below
Outputs:
- local_out: bfloat16 [361, 512, 256], P(None, 'gz', 'xy')
The draws below stay inside these ranges and needn't reach their ends.
Inputs may be any that keep to these rules, and one draw needn't show every extreme that they name: `offsets`: some row is (2, -2) and some row is (-2, 2).
All inputs are finite; a program needn't handle non-finite values.
Results may differ from the reference program's by a relative error of at most 0.0064.
Values may be sent and summed in bfloat16 or wider, within the bound.
No kernel may reach another device: no remote copies, remote signals or barrier semaphores. Data moves between devices by JAX's collectives and lax.ppermute only.
A program may use at most 192 MiB of HBM per device.

```python
import math
import jax
import jax.numpy as jnp
from jax import lax

MC = 361
NE = 648
BY = 8
R = 2
NOFF = 6
NZ = 512
NX = 32
NXY = 256


def draw_offsets(key, part):
    values = jax.random.randint(key, (NOFF, 2), -R, R + 1).astype(jnp.int32)
    values = values.at[0].set(jnp.array([R, -R], jnp.int32))
    values = values.at[1].set(jnp.array([-R, R], jnp.int32))
    return values


def set_ends(drawn, key, low, largest):
    place = [jax.random.randint(jax.random.fold_in(key, axis), (), 0, length) for axis, length in enumerate(drawn.shape)]
    longest = drawn.shape.index(max(drawn.shape))
    next_to = place[:longest] + [(place[longest] + 1) % drawn.shape[longest]] + place[longest + 1:]
    return drawn.at[tuple(place)].set(low).at[tuple(next_to)].set(largest)


def block_scale(rng, shape, shards, smallest, top_value):
    factor_of, own = 1.0, jax.random.fold_in(rng, 6)
    for position, shards_of in shards:
        steps = jnp.exp(jax.random.uniform(jax.random.fold_in(own, position), (shards_of,), jnp.float32, smallest / len(shards), top_value / len(shards)))
        factor_of = factor_of * jnp.repeat(steps, shape[position] // shards_of).reshape([-1 if axis == position else 1 for axis in range(len(shape))])
    return factor_of


def noise(own_key, shape, width, limit, split=(), kind=jnp.bfloat16):
    gain = block_scale(own_key, shape, split, -0.22, 0.18) if split else 1.0
    values = jax.random.normal(own_key, shape, jnp.float32) * width * gain
    return jnp.minimum(jnp.maximum(values, -limit), limit).astype(kind)


def setup_inputs(seed: int = 0) -> dict:
    key_list = jax.random.split(jax.random.key(seed), 9)
    return {
        "moments": noise(key_list[0], (MC, NZ, NXY), 0.3, 4.0, ((1, 64), (2, 2))),
        "counts": set_ends(jax.random.randint(key_list[1], (NZ, NXY), 0, 8), jax.random.fold_in(key_list[1], 1), 0, 7).astype(jnp.int32),
        "m2x": noise(key_list[2], (2 * NE, MC), MC ** -0.5, 0.3125),
        "x2l": noise(key_list[3], (MC, 2 * NE), (2 * NE * NOFF) ** -0.5, 0.0625),
        "decay_rate": jnp.clip(jnp.exp(jax.random.uniform(key_list[4], (NE,), jnp.float32, math.log(0.00048828125), math.log(0.05))), 0.00048828125, 0.05),
        "wave_x": jnp.clip(jax.random.uniform(key_list[5], (NE,), jnp.float32, -3.140625, 3.140625), -3.140625, 3.140625),
        "wave_y": jnp.clip(jax.random.uniform(key_list[6], (NE,), jnp.float32, -3.140625, 3.140625), -3.140625, 3.140625),
        "offsets": draw_offsets(jax.random.fold_in(key_list[8], 71), 0),
    }


def reference(moments, counts, m2x, x2l, decay_rate, wave_x, wave_y, offsets):
    exp_rows = 2 * NE
    rate_col = jnp.concatenate([decay_rate, decay_rate])[:, None]
    factor = jnp.exp(-rate_col)
    weight = jnp.sqrt(1.0 - factor * factor)

    def layer_terms(layer):
        coeff_layer = lax.dynamic_index_in_dim(moments, layer, 1, keepdims=False).astype(jnp.float32)
        count_layer = lax.dynamic_index_in_dim(counts, layer, 0, keepdims=False).astype(jnp.float32)
        multipole = (coeff_layer * count_layer[None, :]).astype(jnp.bfloat16)
        return weight * jnp.dot(m2x, multipole, preferred_element_type=jnp.float32)

    def local_from(upward):
        field_grid = upward.reshape(exp_rows, NX, BY)
        acc_real = jnp.zeros((NE, NX, BY), jnp.float32)
        acc_imag = jnp.zeros((NE, NX, BY), jnp.float32)
        for list_entry in range(NOFF):
            step_x = offsets[list_entry, 0]
            step_y = offsets[list_entry, 1]
            moved = jnp.roll(field_grid, (step_x, step_y), axis=(1, 2))
            phase_angle = wave_x * step_x.astype(jnp.float32) + wave_y * step_y.astype(jnp.float32)
            cosine = jnp.cos(phase_angle)[:, None, None]
            sine_part = jnp.sin(phase_angle)[:, None, None]
            part_real = moved[:NE].astype(jnp.float32)
            part_imag = moved[NE:].astype(jnp.float32)
            acc_real = acc_real + part_real * cosine - part_imag * sine_part
            acc_imag = acc_imag + part_real * sine_part + part_imag * cosine
        shifted = jnp.concatenate([acc_real, acc_imag], axis=0).astype(jnp.bfloat16).reshape(exp_rows, NXY)
        return jnp.dot(x2l, shifted, preferred_element_type=jnp.float32).astype(jnp.bfloat16)

    def first_pass(carry, layer):
        state, prev_term = carry
        fresh = layer_terms(layer)
        return ((factor * state + fresh, fresh), None)
    zero_state = jnp.zeros((exp_rows, NXY), jnp.float32)
    layer_ids = jnp.arange(NZ, dtype=jnp.int32)
    (lap_state, last_term), _ = lax.scan(first_pass, (zero_state, zero_state), layer_ids)
    lap_gain = 1.0 - jnp.exp(-rate_col * NZ)

    def second_pass(carry, layer):
        state, prev_term = carry
        upward = (factor * (state - prev_term)).astype(jnp.bfloat16)
        local_layer = local_from(upward)
        fresh = layer_terms(layer)
        return ((factor * state + fresh, fresh), local_layer)
    _, layer_out = lax.scan(second_pass, (lap_state / lap_gain, last_term), layer_ids)
    return jnp.transpose(layer_out, (1, 0, 2))
```

```python
import jax
import jax.numpy as jnp
from jax import lax
from jax.sharding import PartitionSpec as P

BY = 8
R = 2
NOFF = 6


def from_behind(value, axis, steps):
    count = lax.axis_size(axis)
    pairs = [(source, (source + steps) % count) for source in range(count)]
    return lax.ppermute(value, axis, pairs)


def extended(block, sides, width):
    for axis, dim in sides:
        count = lax.axis_size(axis)
        forward = [(i, i + 1) for i in range(count - 1)]
        forward.append((count - 1, 0))
        backward = [(target, source) for source, target in forward]
        low = lax.ppermute(
            lax.slice_in_dim(block, block.shape[dim] - width, None, axis=dim), axis, forward
        )
        high = lax.ppermute(lax.slice_in_dim(block, 0, width, axis=dim), axis, backward)
        block = jnp.concatenate([low, block, high], axis=dim)
    return block


def entering_sums(outgoing, rate_col, layers):
    rows, boxes = outgoing.shape
    count = lax.axis_size("gz")
    me = lax.axis_index("gz")
    band = -(-rows // count)
    padded = band * count
    held = jnp.pad(outgoing, ((0, padded - rows), (0, 0)))
    held = lax.all_to_all(held, "gz", 0, 0, tiled=True).reshape(count, band, boxes)
    rates = jnp.pad(rate_col[:, 0], (0, padded - rows), constant_values=1.0)
    my_rates = lax.dynamic_slice_in_dim(rates, me * band, band)
    slab = jnp.arange(count, dtype=jnp.int32)
    gap = (slab[:, None] - 1 - slab[None, :]) % count
    weights = jnp.exp(-my_rates[:, None, None] * (layers * gap.astype(jnp.float32))[None])
    weights = weights / (1.0 - jnp.exp(-my_rates * (layers * count)))[:, None, None]
    sums = jnp.einsum("rst,trb->srb", weights, held, precision=lax.Precision.HIGHEST)
    sums = lax.all_to_all(sums.reshape(padded, boxes), "gz", 0, 0, tiled=True)
    return sums[:rows]


def build_upward(box_terms, entering, before_term, rate_col, factor):
    layers = box_terms.shape[1]
    layer_pos = jnp.arange(layers, dtype=jnp.float32)
    layer_gap = layer_pos[:, None] - layer_pos[None, :]
    decay_table = jnp.where(
        layer_gap[None] >= 2.0,
        jnp.exp(-rate_col[:, :, None] * jnp.maximum(layer_gap, 0.0)[None]),
        0.0,
    )
    upward = jnp.einsum("kij,kjb->kib", decay_table, box_terms, precision=lax.Precision.HIGHEST)
    first = (layer_pos == 0.0)[None, :, None]
    upward = (
        upward
        + jnp.exp(-rate_col * (layer_pos + 1.0)[None, :])[:, :, None] * entering[:, None, :]
        - jnp.where(first, factor[:, :, None] * before_term[:, None, :], 0.0)
    )
    return upward


def body(moments, counts, m2x, x2l, decay_rate, wave_x, wave_y, offsets):
    coeffs, layers, plane_size = moments.shape
    exp_rows = m2x.shape[0]
    half_rows = exp_rows // 2
    columns = plane_size // BY
    rate_col = jnp.concatenate([decay_rate, decay_rate])[:, None]
    factor = jnp.exp(-rate_col)
    weight = jnp.sqrt(1.0 - factor * factor)
    multipole = (moments.astype(jnp.float32) * counts.astype(jnp.float32)[None]).astype(
        jnp.bfloat16
    )
    expansion = jnp.dot(
        m2x, multipole.reshape(coeffs, layers * plane_size), preferred_element_type=jnp.float32
    )
    box_terms = (weight * expansion).reshape(exp_rows, layers, plane_size)
    layer_pos = jnp.arange(layers, dtype=jnp.float32)
    tail_power = jnp.exp(-rate_col * (layers - 1.0 - layer_pos)[None, :])
    outgoing = jnp.einsum("kz,kzb->kb", tail_power, box_terms, precision=lax.Precision.HIGHEST)
    before_term = from_behind(box_terms[:, layers - 1, :].astype(jnp.bfloat16), "gz", 1).astype(
        jnp.float32
    )
    entering = entering_sums(outgoing, rate_col, float(layers))
    upward = build_upward(box_terms, entering, before_term, rate_col, factor)
    field_grid = upward.astype(jnp.bfloat16).reshape(exp_rows, layers, columns, BY)
    padded = extended(field_grid, (("xy", 2),), R)
    acc_real = jnp.zeros((half_rows, layers, columns, BY), jnp.float32)
    acc_imag = jnp.zeros((half_rows, layers, columns, BY), jnp.float32)
    for list_entry in range(NOFF):
        step_x = offsets[list_entry, 0]
        step_y = offsets[list_entry, 1]
        moved = lax.dynamic_slice_in_dim(padded, R - step_x, columns, 2)
        moved = jnp.roll(moved, step_y, axis=3)
        phase_angle = wave_x * step_x.astype(jnp.float32) + wave_y * step_y.astype(jnp.float32)
        cosine = jnp.cos(phase_angle)[:, None, None, None]
        sine_part = jnp.sin(phase_angle)[:, None, None, None]
        part_real = moved[:half_rows].astype(jnp.float32)
        part_imag = moved[half_rows:].astype(jnp.float32)
        acc_real = acc_real + part_real * cosine - part_imag * sine_part
        acc_imag = acc_imag + part_real * sine_part + part_imag * cosine
    shifted = (
        jnp.concatenate([acc_real, acc_imag], axis=0)
        .astype(jnp.bfloat16)
        .reshape(exp_rows, layers * plane_size)
    )
    local_out = jnp.dot(x2l, shifted, preferred_element_type=jnp.float32).astype(jnp.bfloat16)
    return local_out.reshape(coeffs, layers, plane_size)


def solution(mesh):
    in_specs = (P(None, "gz", "xy"), P("gz", "xy"), P(), P(), P(), P(), P(), P())
    out_specs = P(None, "gz", "xy")
    return jax.shard_map(body, mesh=mesh, in_specs=in_specs, out_specs=out_specs, check_vma=False)
```

```python
import jax
import jax.numpy as jnp
from jax import lax
from jax.sharding import PartitionSpec as P

BY = 8
R = 2
NOFF = 6


def from_behind(value, axis, steps):
    count = lax.axis_size(axis)
    pairs = [(source, (source + steps) % count) for source in range(count)]
    return lax.ppermute(value, axis, pairs)


def with_halo(block, axis, dim, width):
    low = from_behind(lax.slice_in_dim(block, block.shape[dim] - width, None, axis=dim), axis, 1)
    high = from_behind(lax.slice_in_dim(block, 0, width, axis=dim), axis, -1)
    return jnp.concatenate([low, block, high], axis=dim)


def entering_sums(outgoing, rate_rows, layers):
    rows, boxes = outgoing.shape
    count = lax.axis_size("gz")
    me = lax.axis_index("gz")
    band = -(-rows // count)
    padded = band * count
    held = jnp.pad(outgoing, ((0, padded - rows), (0, 0)))
    held = lax.all_to_all(held, "gz", 0, 0, tiled=True).reshape(count, band, boxes)
    rates = jnp.pad(rate_rows, (0, padded - rows), constant_values=1.0)
    my_rates = lax.dynamic_slice_in_dim(rates, me * band, band)
    slab = jnp.arange(count, dtype=jnp.int32)
    gap = (slab[:, None] - 1 - slab[None, :]) % count
    weights = jnp.exp(-my_rates[:, None, None] * (layers * gap.astype(jnp.float32))[None])
    weights = weights / (1.0 - jnp.exp(-my_rates * (layers * count)))[:, None, None]
    sums = jnp.einsum("rst,trb->srb", weights, held, precision=lax.Precision.HIGHEST)
    sums = lax.all_to_all(sums.reshape(padded, boxes), "gz", 0, 0, tiled=True)
    return sums[:rows]


def body(moments, counts, m2x, x2l, decay_rate, wave_x, wave_y, offsets):
    coeffs, layers, plane_size = moments.shape
    exp_rows = m2x.shape[0]
    half_rows = exp_rows // 2
    columns = plane_size // BY
    ext_columns = columns + 2 * R
    ext_boxes = ext_columns * BY
    rate = decay_rate[None, None, :]
    factor = jnp.exp(-rate)
    weight = jnp.sqrt(1.0 - factor * factor)
    multipole = (moments.astype(jnp.float32) * counts.astype(jnp.float32)[None]).astype(
        jnp.bfloat16
    )
    multipole = with_halo(multipole, "xy", 2, R * BY)
    by_box = jnp.transpose(multipole, (0, 2, 1)).reshape(coeffs, ext_boxes * layers)
    expansion = jnp.einsum(
        "pkc,cn->pnk",
        m2x.reshape(2, half_rows, coeffs),
        by_box,
        preferred_element_type=jnp.float32,
    )
    box_terms = (weight * expansion).reshape(2, ext_boxes, layers, half_rows)

    outgoing = box_terms[:, :, layers - 1, :]
    for j in range(layers - 1):
        outgoing = outgoing + jnp.exp(-rate * float(layers - 1 - j)) * box_terms[:, :, j, :]
    before_term = from_behind(box_terms[:, :, layers - 1, :], "gz", 1)

    rows_out = jnp.transpose(outgoing, (0, 2, 1)).reshape(exp_rows, ext_boxes)
    entering = entering_sums(rows_out, jnp.concatenate([decay_rate, decay_rate]), float(layers))
    entering = jnp.transpose(entering.reshape(2, half_rows, ext_boxes), (0, 2, 1))

    layer_pos = jnp.arange(layers, dtype=jnp.float32)[None, None, :, None]
    upward = jnp.exp(-rate[:, :, None, :] * (layer_pos + 1.0)) * entering[:, :, None, :]
    for j in range(layers - 2):
        gap = layer_pos - float(j)
        coeff = jnp.where(gap >= 2.0, jnp.exp(-rate[:, :, None, :] * jnp.maximum(gap, 0.0)), 0.0)
        upward = upward + coeff * box_terms[:, :, j : j + 1, :]
    first = layer_pos == 0.0
    upward = upward - jnp.where(first, factor[:, :, None, :] * before_term[:, :, None, :], 0.0)

    field = upward.astype(jnp.bfloat16).reshape(2, ext_columns, BY, layers, half_rows)
    field = jnp.concatenate([field[:, :, BY - R :], field, field[:, :, :R]], axis=2)
    acc_real = jnp.zeros((columns, BY, layers, half_rows), jnp.float32)
    acc_imag = jnp.zeros((columns, BY, layers, half_rows), jnp.float32)
    for list_entry in range(NOFF):
        step_x = offsets[list_entry, 0]
        step_y = offsets[list_entry, 1]
        moved = lax.dynamic_slice(
            field, (0, R - step_x, R - step_y, 0, 0), (2, columns, BY, layers, half_rows)
        )
        phase_angle = wave_x * step_x.astype(jnp.float32) + wave_y * step_y.astype(jnp.float32)
        cosine = jnp.cos(phase_angle)
        sine_part = jnp.sin(phase_angle)
        part_real = moved[0].astype(jnp.float32)
        part_imag = moved[1].astype(jnp.float32)
        acc_real = acc_real + part_real * cosine - part_imag * sine_part
        acc_imag = acc_imag + part_real * sine_part + part_imag * cosine
    shifted = jnp.stack([acc_real, acc_imag]).astype(jnp.bfloat16)
    shifted = shifted.reshape(2, columns * BY * layers, half_rows)
    local_out = jnp.einsum(
        "cpk,pnk->cn",
        x2l.reshape(coeffs, 2, half_rows),
        shifted,
        preferred_element_type=jnp.float32,
    ).astype(jnp.bfloat16)
    local_out = local_out.reshape(coeffs, plane_size, layers)
    return jnp.transpose(local_out, (0, 2, 1))


def solution(mesh):
    in_specs = (P(None, "gz", "xy"), P("gz", "xy"), P(), P(), P(), P(), P(), P())
    out_specs = P(None, "gz", "xy")
    return jax.shard_map(body, mesh=mesh, in_specs=in_specs, out_specs=out_specs, check_vma=False)
```

```python
import jax
import jax.numpy as jnp
from jax import lax
from jax.sharding import PartitionSpec as P

BY = 8
R = 2
NOFF = 6
TILE_ROWS = 16
TILE = TILE_ROWS * 256


def from_behind(value, axis, steps):
    count = lax.axis_size(axis)
    pairs = [(source, (source + steps) % count) for source in range(count)]
    return lax.ppermute(value, axis, pairs)


def with_halo(block, axis, dim, width):
    low = from_behind(lax.slice_in_dim(block, block.shape[dim] - width, None, axis=dim), axis, 1)
    high = from_behind(lax.slice_in_dim(block, 0, width, axis=dim), axis, -1)
    return jnp.concatenate([low, block, high], axis=dim)


def cyclic_decayed_sum(held, gain_of):
    count = held.shape[0]
    result, offset, span, block, left = None, 0, 1, held, count
    while left:
        if left & 1:
            term = jnp.roll(block, offset, axis=0)
            if offset:
                term = gain_of(offset) * term
            result = term if result is None else result + term
            offset += span
        left >>= 1
        if left:
            block = block + gain_of(span) * jnp.roll(block, span, axis=0)
            span *= 2
    return result


def entering_sums(outgoing, rate_full, layers):
    shape = outgoing.shape
    size = outgoing.size
    count = lax.axis_size("gz")
    me = lax.axis_index("gz")
    chunk = -(-size // (count * TILE)) * TILE
    padded = chunk * count

    def spread(values, fill):
        flat = jnp.pad(values.reshape(-1), (0, padded - size), constant_values=fill)
        return flat.reshape(count, TILE_ROWS, chunk // TILE_ROWS)

    held = lax.all_to_all(spread(outgoing.astype(jnp.bfloat16), 0), "gz", 0, 0, tiled=True)
    held = held.reshape(count, chunk).astype(jnp.float32)
    my_rates = lax.dynamic_index_in_dim(spread(rate_full, 1.0).reshape(count, chunk), me, 0, False)
    sums = cyclic_decayed_sum(held, lambda steps: jnp.exp(-my_rates * (layers * steps)))
    sums = jnp.roll(sums, 1, axis=0) / (1.0 - jnp.exp(-my_rates * (layers * count)))
    sums = sums.astype(jnp.bfloat16).reshape(count, TILE_ROWS, chunk // TILE_ROWS)
    back = lax.all_to_all(sums, "gz", 0, 0, tiled=True)
    return back.reshape(-1)[:size].reshape(shape).astype(jnp.float32)


def body(moments, counts, m2x, x2l, decay_rate, wave_x, wave_y, offsets):
    coeffs, layers, plane_size = moments.shape
    exp_rows = m2x.shape[0]
    half_rows = exp_rows // 2
    columns = plane_size // BY
    ext_columns = columns + 2 * R
    ext_boxes = ext_columns * BY
    rate = decay_rate[None, None, None, :]
    factor = jnp.exp(-rate)
    weight = jnp.sqrt(1.0 - factor * factor)
    multipole = (moments.astype(jnp.float32) * counts.astype(jnp.float32)[None]).astype(
        jnp.bfloat16
    )
    multipole = with_halo(multipole, "xy", 2, R * BY).reshape(coeffs, layers * ext_boxes)
    halves = []
    for part in range(2):
        rows = m2x[part * half_rows : (part + 1) * half_rows]
        expansion = lax.dot_general(
            multipole, rows, (((0,), (1,)), ((), ())), preferred_element_type=jnp.float32
        )
        halves.append(expansion.reshape(layers, ext_boxes, half_rows))
    box_terms = weight * jnp.stack(halves)

    outgoing = box_terms[:, layers - 1]
    for j in range(layers - 1):
        outgoing = outgoing + jnp.exp(-rate[0] * float(layers - 1 - j)) * box_terms[:, j]
    outgoing, box_terms = lax.optimization_barrier((outgoing, box_terms))
    before_term = from_behind(box_terms[:, layers - 1].astype(jnp.bfloat16), "gz", 1)

    rate_full = jnp.broadcast_to(decay_rate, outgoing.shape)
    entering = entering_sums(outgoing, rate_full, float(layers))

    layer_pos = jnp.arange(layers, dtype=jnp.float32)[None, :, None, None]
    upward = jnp.exp(-rate * (layer_pos + 1.0)) * entering[:, None]
    for j in range(layers - 2):
        gap = layer_pos - float(j)
        coeff = jnp.where(gap >= 2.0, jnp.exp(-rate * jnp.maximum(gap, 0.0)), 0.0)
        upward = upward + coeff * box_terms[:, j : j + 1]
    first = layer_pos == 0.0
    upward = upward - jnp.where(first, factor * before_term[:, None].astype(jnp.float32), 0.0)

    field = upward.astype(jnp.bfloat16).reshape(2, layers, ext_columns, BY, half_rows)
    field = jnp.transpose(field, (0, 2, 3, 1, 4))
    field = jnp.concatenate([field[:, :, BY - R :], field, field[:, :, :R]], axis=2)
    acc_real = jnp.zeros((columns, BY, layers, half_rows), jnp.float32)
    acc_imag = jnp.zeros((columns, BY, layers, half_rows), jnp.float32)
    for list_entry in range(NOFF):
        step_x = offsets[list_entry, 0]
        step_y = offsets[list_entry, 1]
        moved = lax.dynamic_slice(
            field, (0, R - step_x, R - step_y, 0, 0), (2, columns, BY, layers, half_rows)
        )
        phase_angle = wave_x * step_x.astype(jnp.float32) + wave_y * step_y.astype(jnp.float32)
        cosine = jnp.cos(phase_angle)
        sine_part = jnp.sin(phase_angle)
        part_real = moved[0].astype(jnp.float32)
        part_imag = moved[1].astype(jnp.float32)
        acc_real = acc_real + part_real * cosine - part_imag * sine_part
        acc_imag = acc_imag + part_real * sine_part + part_imag * cosine
    local_out = None
    for part, acc in enumerate((acc_real, acc_imag)):
        shifted = acc.astype(jnp.bfloat16).reshape(columns * BY * layers, half_rows)
        product = lax.dot_general(
            x2l[:, part * half_rows : (part + 1) * half_rows],
            shifted,
            (((1,), (1,)), ((), ())),
            preferred_element_type=jnp.float32,
        )
        local_out = product if local_out is None else local_out + product
    local_out = local_out.astype(jnp.bfloat16).reshape(coeffs, columns, BY, layers)
    return jnp.transpose(local_out, (0, 3, 1, 2)).reshape(coeffs, layers, plane_size)


def solution(mesh):
    in_specs = (P(None, "gz", "xy"), P("gz", "xy"), P(), P(), P(), P(), P(), P())
    out_specs = P(None, "gz", "xy")
    return jax.shard_map(body, mesh=mesh, in_specs=in_specs, out_specs=out_specs, check_vma=False)
```

```python
import jax
import jax.numpy as jnp
from jax import lax
from jax.sharding import PartitionSpec as P

BY = 8
R = 2
NOFF = 6
TILE_ROWS = 8
TILE = TILE_ROWS * 128


def from_behind(value, axis, steps):
    count = lax.axis_size(axis)
    pairs = [(source, (source + steps) % count) for source in range(count)]
    return lax.ppermute(value, axis, pairs)


def cyclic_decayed_sum(held, gain_of):
    count = held.shape[0]
    result, offset, span, block, left = None, 0, 1, held, count
    while left:
        if left & 1:
            term = jnp.roll(block, offset, axis=0)
            if offset:
                term = gain_of(offset) * term
            result = term if result is None else result + term
            offset += span
        left >>= 1
        if left:
            block = block + gain_of(span) * jnp.roll(block, span, axis=0)
            span *= 2
    return result


def entering_sums(outgoing, rate_full, layers):
    shape = outgoing.shape
    size = outgoing.size
    count = lax.axis_size("gz")
    me = lax.axis_index("gz")
    chunk = -(-size // (count * TILE)) * TILE
    padded = chunk * count

    def spread(values, fill):
        flat = jnp.pad(values.reshape(-1), (0, padded - size), constant_values=fill)
        return flat.reshape(count, TILE_ROWS, chunk // TILE_ROWS)

    held = lax.all_to_all(spread(outgoing, 0.0), "gz", 0, 0, tiled=True)
    held = held.reshape(count, chunk)
    my_rates = lax.dynamic_index_in_dim(spread(rate_full, 1.0).reshape(count, chunk), me, 0, False)
    sums = cyclic_decayed_sum(held, lambda steps: jnp.exp(-my_rates * (layers * steps)))
    sums = jnp.roll(sums, 1, axis=0) / (1.0 - jnp.exp(-my_rates * (layers * count)))
    sums = sums.reshape(count, TILE_ROWS, chunk // TILE_ROWS)
    back = lax.all_to_all(sums, "gz", 0, 0, tiled=True)
    return back.reshape(-1)[:size].reshape(shape)


def decayed_upward(box_terms, entering, before_term, rate, factor):
    layers = box_terms.shape[1]
    layer_pos = jnp.arange(layers, dtype=jnp.float32)[None, :, None, None]
    upward = jnp.exp(-rate * (layer_pos + 1.0)) * entering[:, None]
    for j in range(layers - 2):
        gap = layer_pos - float(j)
        coeff = jnp.where(gap >= 2.0, jnp.exp(-rate * jnp.maximum(gap, 0.0)), 0.0)
        upward = upward + coeff * box_terms[:, j : j + 1]
    first = layer_pos == 0.0
    return upward - jnp.where(first, factor * before_term[:, None].astype(jnp.float32), 0.0)


def expand(multipole, m2x, weight):
    coeffs, layers, boxes = multipole.shape
    half_rows = m2x.shape[0] // 2
    flat = multipole.reshape(coeffs, layers * boxes)
    halves = []
    for part in range(2):
        rows = m2x[part * half_rows : (part + 1) * half_rows]
        expansion = lax.dot_general(
            flat, rows, (((0,), (1,)), ((), ())), preferred_element_type=jnp.float32
        )
        halves.append(expansion.reshape(layers, boxes, half_rows))
    return weight * jnp.stack(halves)


def body(moments, counts, m2x, x2l, decay_rate, wave_x, wave_y, offsets):
    coeffs, layers, plane_size = moments.shape
    exp_rows = m2x.shape[0]
    half_rows = exp_rows // 2
    columns = plane_size // BY
    ext_columns = columns + 2 * R
    width = R * BY
    rate = decay_rate[None, None, None, :]
    factor = jnp.exp(-rate)
    weight = jnp.sqrt(1.0 - factor * factor)
    multipole = (moments.astype(jnp.float32) * counts.astype(jnp.float32)[None]).astype(
        jnp.bfloat16
    )
    halo_low = from_behind(multipole[:, :, plane_size - width :], "xy", 1)
    halo_high = from_behind(multipole[:, :, :width], "xy", -1)
    box_terms = expand(multipole, m2x, weight)
    halo_terms = expand(jnp.concatenate([halo_low, halo_high], axis=2), m2x, weight)

    outgoing = box_terms[:, layers - 1]
    for j in range(layers - 1):
        outgoing = outgoing + jnp.exp(-rate[0] * float(layers - 1 - j)) * box_terms[:, j]
    outgoing, box_terms = lax.optimization_barrier((outgoing, box_terms))
    before_term = from_behind(box_terms[:, layers - 1].astype(jnp.bfloat16), "gz", 1)
    halo_before = from_behind(halo_terms[:, layers - 1].astype(jnp.bfloat16), "gz", 1)

    rate_full = jnp.broadcast_to(decay_rate, outgoing.shape)
    entering = entering_sums(outgoing, rate_full, float(layers))
    entering_low = from_behind(entering[:, plane_size - width :], "xy", 1)
    entering_high = from_behind(entering[:, :width], "xy", -1)
    halo_entering = jnp.concatenate([entering_low, entering_high], axis=1)

    upward = decayed_upward(box_terms, entering, before_term, rate, factor)
    halo_upward = decayed_upward(halo_terms, halo_entering, halo_before, rate, factor)
    upward = jnp.concatenate(
        [halo_upward[:, :, :width], upward, halo_upward[:, :, width:]], axis=2
    )

    field = upward.astype(jnp.bfloat16).reshape(2, layers, ext_columns, BY, half_rows)
    field = jnp.transpose(field, (0, 2, 3, 1, 4))
    field = jnp.concatenate([field[:, :, BY - R :], field, field[:, :, :R]], axis=2)
    acc_real = jnp.zeros((columns, BY, layers, half_rows), jnp.float32)
    acc_imag = jnp.zeros((columns, BY, layers, half_rows), jnp.float32)
    for list_entry in range(NOFF):
        step_x = offsets[list_entry, 0]
        step_y = offsets[list_entry, 1]
        moved = lax.dynamic_slice(
            field, (0, R - step_x, R - step_y, 0, 0), (2, columns, BY, layers, half_rows)
        )
        phase_angle = wave_x * step_x.astype(jnp.float32) + wave_y * step_y.astype(jnp.float32)
        cosine = jnp.cos(phase_angle)
        sine_part = jnp.sin(phase_angle)
        part_real = moved[0].astype(jnp.float32)
        part_imag = moved[1].astype(jnp.float32)
        acc_real = acc_real + part_real * cosine - part_imag * sine_part
        acc_imag = acc_imag + part_real * sine_part + part_imag * cosine
    local_out = None
    for part, acc in enumerate((acc_real, acc_imag)):
        shifted = acc.astype(jnp.bfloat16).reshape(columns * BY * layers, half_rows)
        product = lax.dot_general(
            x2l[:, part * half_rows : (part + 1) * half_rows],
            shifted,
            (((1,), (1,)), ((), ())),
            preferred_element_type=jnp.float32,
        )
        local_out = product if local_out is None else local_out + product
    local_out = local_out.astype(jnp.bfloat16).reshape(coeffs, columns, BY, layers)
    return jnp.transpose(local_out, (0, 3, 1, 2)).reshape(coeffs, layers, plane_size)


def solution(mesh):
    in_specs = (P(None, "gz", "xy"), P("gz", "xy"), P(), P(), P(), P(), P(), P())
    out_specs = P(None, "gz", "xy")
    return jax.shard_map(body, mesh=mesh, in_specs=in_specs, out_specs=out_specs, check_vma=False)
```

```python
import jax
import jax.numpy as jnp
from jax import lax
from jax.sharding import PartitionSpec as P

BY = 8
R = 2
NOFF = 6
TILE_ROWS = 8
TILE = TILE_ROWS * 512


def from_behind(value, axis, steps):
    count = lax.axis_size(axis)
    pairs = [(source, (source + steps) % count) for source in range(count)]
    return lax.ppermute(value, axis, pairs)


def with_halo(block, axis, dim, width):
    low = from_behind(lax.slice_in_dim(block, block.shape[dim] - width, None, axis=dim), axis, 1)
    high = from_behind(lax.slice_in_dim(block, 0, width, axis=dim), axis, -1)
    return jnp.concatenate([low, block, high], axis=dim)


def cyclic_decayed_sum(held, gain_of):
    count = held.shape[0]
    result, offset, span, block, left = None, 0, 1, held, count
    while left:
        if left & 1:
            term = jnp.roll(block, offset, axis=0)
            if offset:
                term = gain_of(offset) * term
            result = term if result is None else result + term
            offset += span
        left >>= 1
        if left:
            block = block + gain_of(span) * jnp.roll(block, span, axis=0)
            span *= 2
    return result


def entering_sums(outgoing, rate_full, layers):
    shape = outgoing.shape
    size = outgoing.size
    count = lax.axis_size("gz")
    me = lax.axis_index("gz")
    chunk = -(-size // (count * TILE)) * TILE
    padded = chunk * count

    def spread(values, fill):
        flat = jnp.pad(values.reshape(-1), (0, padded - size), constant_values=fill)
        return flat.reshape(count, TILE_ROWS, chunk // TILE_ROWS)

    held = lax.all_to_all(spread(outgoing, 0.0), "gz", 0, 0, tiled=True)
    held = held.reshape(count, chunk)
    my_rates = lax.dynamic_index_in_dim(spread(rate_full, 1.0).reshape(count, chunk), me, 0, False)
    sums = cyclic_decayed_sum(held, lambda steps: jnp.exp(-my_rates * (layers * steps)))
    sums = jnp.roll(sums, 1, axis=0) / (1.0 - jnp.exp(-my_rates * (layers * count)))
    sums = sums.reshape(count, TILE_ROWS, chunk // TILE_ROWS)
    back = lax.all_to_all(sums, "gz", 0, 0, tiled=True)
    return back.reshape(-1)[:size].reshape(shape)


def body(moments, counts, m2x, x2l, decay_rate, wave_x, wave_y, offsets):
    coeffs, layers, plane_size = moments.shape
    exp_rows = m2x.shape[0]
    half_rows = exp_rows // 2
    columns = plane_size // BY
    ext_columns = columns + 2 * R
    ext_boxes = ext_columns * BY
    rate = decay_rate[None, None, None, :]
    factor = jnp.exp(-rate)
    weight = jnp.sqrt(1.0 - factor * factor)
    multipole = (moments.astype(jnp.float32) * counts.astype(jnp.float32)[None]).astype(
        jnp.bfloat16
    )
    multipole = with_halo(multipole, "xy", 2, R * BY).reshape(coeffs, layers * ext_boxes)
    halves = []
    for part in range(2):
        rows = m2x[part * half_rows : (part + 1) * half_rows]
        expansion = lax.dot_general(
            multipole, rows, (((0,), (1,)), ((), ())), preferred_element_type=jnp.float32
        )
        halves.append(expansion.reshape(layers, ext_boxes, half_rows))
    box_terms = weight * jnp.stack(halves)

    outgoing = box_terms[:, layers - 1]
    for j in range(layers - 1):
        outgoing = outgoing + jnp.exp(-rate[0] * float(layers - 1 - j)) * box_terms[:, j]
    outgoing, box_terms = lax.optimization_barrier((outgoing, box_terms))
    before_term = from_behind(box_terms[:, layers - 1].astype(jnp.bfloat16), "gz", 1)

    rate_full = jnp.broadcast_to(decay_rate, outgoing.shape)
    entering = entering_sums(outgoing, rate_full, float(layers))

    layer_pos = jnp.arange(layers, dtype=jnp.float32)[None, :, None, None]
    upward = jnp.exp(-rate * (layer_pos + 1.0)) * entering[:, None]
    for j in range(layers - 2):
        gap = layer_pos - float(j)
        coeff = jnp.where(gap >= 2.0, jnp.exp(-rate * jnp.maximum(gap, 0.0)), 0.0)
        upward = upward + coeff * box_terms[:, j : j + 1]
    first = layer_pos == 0.0
    upward = upward - jnp.where(first, factor * before_term[:, None].astype(jnp.float32), 0.0)

    field = upward.astype(jnp.bfloat16).reshape(2, layers, ext_columns, BY, half_rows)
    field = jnp.transpose(field, (0, 2, 3, 1, 4))
    field = jnp.concatenate([field[:, :, BY - R :], field, field[:, :, :R]], axis=2)
    acc_real = jnp.zeros((columns, BY, layers, half_rows), jnp.float32)
    acc_imag = jnp.zeros((columns, BY, layers, half_rows), jnp.float32)
    for list_entry in range(NOFF):
        step_x = offsets[list_entry, 0]
        step_y = offsets[list_entry, 1]
        moved = lax.dynamic_slice(
            field, (0, R - step_x, R - step_y, 0, 0), (2, columns, BY, layers, half_rows)
        )
        phase_angle = wave_x * step_x.astype(jnp.float32) + wave_y * step_y.astype(jnp.float32)
        cosine = jnp.cos(phase_angle)
        sine_part = jnp.sin(phase_angle)
        part_real = moved[0].astype(jnp.float32)
        part_imag = moved[1].astype(jnp.float32)
        acc_real = acc_real + part_real * cosine - part_imag * sine_part
        acc_imag = acc_imag + part_real * sine_part + part_imag * cosine
    local_out = None
    for part, acc in enumerate((acc_real, acc_imag)):
        shifted = acc.astype(jnp.bfloat16).reshape(columns * BY * layers, half_rows)
        product = lax.dot_general(
            x2l[:, part * half_rows : (part + 1) * half_rows],
            shifted,
            (((1,), (1,)), ((), ())),
            preferred_element_type=jnp.float32,
        )
        local_out = product if local_out is None else local_out + product
    local_out = local_out.astype(jnp.bfloat16).reshape(coeffs, columns, BY, layers)
    return jnp.transpose(local_out, (0, 3, 1, 2)).reshape(coeffs, layers, plane_size)


def solution(mesh):
    in_specs = (P(None, "gz", "xy"), P("gz", "xy"), P(), P(), P(), P(), P(), P())
    out_specs = P(None, "gz", "xy")
    return jax.shard_map(body, mesh=mesh, in_specs=in_specs, out_specs=out_specs, check_vma=False)
```

```python
import jax
import jax.numpy as jnp
from jax import lax
from jax.experimental import pallas as pl
from jax.experimental.pallas import tpu as pltpu
from jax.sharding import PartitionSpec as P

BY = 8
R = 2
NOFF = 6
TILE_ROWS = 8
TILE = TILE_ROWS * 512


def from_behind(value, axis, steps):
    count = lax.axis_size(axis)
    pairs = [(source, (source + steps) % count) for source in range(count)]
    return lax.ppermute(value, axis, pairs)


def with_halo(block, axis, dim, width):
    low = from_behind(lax.slice_in_dim(block, block.shape[dim] - width, None, axis=dim), axis, 1)
    high = from_behind(lax.slice_in_dim(block, 0, width, axis=dim), axis, -1)
    return jnp.concatenate([low, block, high], axis=dim)


def cyclic_decayed_sum(held, gain_of):
    count = held.shape[0]
    result, offset, span, block, left = None, 0, 1, held, count
    while left:
        if left & 1:
            term = jnp.roll(block, offset, axis=0)
            if offset:
                term = gain_of(offset) * term
            result = term if result is None else result + term
            offset += span
        left >>= 1
        if left:
            block = block + gain_of(span) * jnp.roll(block, span, axis=0)
            span *= 2
    return result


def entering_sums(outgoing, rate_full, layers):
    shape = outgoing.shape
    size = outgoing.size
    count = lax.axis_size("gz")
    me = lax.axis_index("gz")
    chunk = -(-size // (count * TILE)) * TILE
    padded = chunk * count

    def spread(values, fill):
        flat = jnp.pad(values.reshape(-1), (0, padded - size), constant_values=fill)
        return flat.reshape(count, TILE_ROWS, chunk // TILE_ROWS)

    held = lax.all_to_all(spread(outgoing, 0.0), "gz", 0, 0, tiled=True)
    held = held.reshape(count, chunk)
    my_rates = lax.dynamic_index_in_dim(spread(rate_full, 1.0).reshape(count, chunk), me, 0, False)
    sums = cyclic_decayed_sum(held, lambda steps: jnp.exp(-my_rates * (layers * steps)))
    sums = jnp.roll(sums, 1, axis=0) / (1.0 - jnp.exp(-my_rates * (layers * count)))
    sums = sums.reshape(count, TILE_ROWS, chunk // TILE_ROWS)
    back = lax.all_to_all(sums, "gz", 0, 0, tiled=True)
    return back.reshape(-1)[:size].reshape(shape)


def shift_kernel(steps_ref, terms_ref, entering_ref, before_ref, coef_ref, lift_ref, factor_ref,
                 cos_ref, sin_ref, out_ref, field_ref):
    _, layers, boxes, width = terms_ref.shape
    _, _, columns, rows, _ = out_ref.shape
    for i in range(layers):
        up = lift_ref[i] * entering_ref[...]
        for j in range(i - 1):
            up = up + coef_ref[i, j] * terms_ref[:, j]
        if i == 0:
            up = up - factor_ref[...] * before_ref[...].astype(jnp.float32)
        up = up.astype(jnp.bfloat16).astype(jnp.float32)
        field_ref[...] = up.reshape(2, boxes // rows, rows, width)
        acc_real = jnp.zeros((columns, rows, width), jnp.float32)
        acc_imag = jnp.zeros((columns, rows, width), jnp.float32)
        for entry in range(NOFF):
            start = jnp.clip(R - steps_ref[entry, 0], 0, 2 * R)
            turn = lax.rem(steps_ref[entry, 1] + rows, rows)
            moved = field_ref[:, pl.ds(start, columns), :, :]
            moved = pltpu.roll(moved, turn, 2)
            cosine = cos_ref[entry]
            sine_part = sin_ref[entry]
            acc_real = acc_real + moved[0] * cosine - moved[1] * sine_part
            acc_imag = acc_imag + moved[0] * sine_part + moved[1] * cosine
        out_ref[0, i] = acc_real.astype(out_ref.dtype)
        out_ref[1, i] = acc_imag.astype(out_ref.dtype)


def shift_layers(offsets, box_terms, entering, before_term, rate, wave_x, wave_y, columns):
    _, layers, boxes, width = box_terms.shape
    layer_pos = jnp.arange(layers, dtype=jnp.float32)
    gap = layer_pos[:, None] - layer_pos[None, :]
    coef = jnp.where(
        gap[:, :, None] >= 2.0, jnp.exp(-rate * jnp.maximum(gap, 0.0)[:, :, None]), 0.0
    )[:, :, None, :]
    lift = jnp.exp(-rate * (layer_pos + 1.0)[:, None])[:, None, :]
    factor = jnp.exp(-rate)[None, :]
    steps = offsets.astype(jnp.float32)
    phase_angle = steps[:, :1] * wave_x[None] + steps[:, 1:] * wave_y[None]
    vmem = pl.BlockSpec(memory_space=pltpu.VMEM)
    smem = pl.BlockSpec(memory_space=pltpu.SMEM)
    return pl.pallas_call(
        shift_kernel,
        out_shape=jax.ShapeDtypeStruct((2, layers, columns, BY, width), jnp.bfloat16),
        in_specs=[smem] + [vmem] * 8,
        out_specs=vmem,
        scratch_shapes=[pltpu.VMEM((2, boxes // BY, BY, width), jnp.float32)],
        cost_estimate=pl.CostEstimate(
            flops=2 * layers * boxes * width * 40,
            transcendentals=0,
            bytes_accessed=box_terms.size * 4 + 3 * entering.size * 4,
        ),
    )(offsets, box_terms, entering, before_term, coef, lift, factor,
      jnp.cos(phase_angle)[:, None, :], jnp.sin(phase_angle)[:, None, :])


def body(moments, counts, m2x, x2l, decay_rate, wave_x, wave_y, offsets):
    coeffs, layers, plane_size = moments.shape
    exp_rows = m2x.shape[0]
    half_rows = exp_rows // 2
    columns = plane_size // BY
    ext_columns = columns + 2 * R
    ext_boxes = ext_columns * BY
    rate = decay_rate[None, None, None, :]
    factor = jnp.exp(-rate)
    weight = jnp.sqrt(1.0 - factor * factor)
    multipole = (moments.astype(jnp.float32) * counts.astype(jnp.float32)[None]).astype(
        jnp.bfloat16
    )
    multipole = with_halo(multipole, "xy", 2, R * BY).reshape(coeffs, layers * ext_boxes)
    halves = []
    for part in range(2):
        rows = m2x[part * half_rows : (part + 1) * half_rows]
        expansion = lax.dot_general(
            multipole, rows, (((0,), (1,)), ((), ())), preferred_element_type=jnp.float32
        )
        halves.append(expansion.reshape(layers, ext_boxes, half_rows))
    box_terms = weight * jnp.stack(halves)

    outgoing = box_terms[:, layers - 1]
    for j in range(layers - 1):
        outgoing = outgoing + jnp.exp(-rate[0] * float(layers - 1 - j)) * box_terms[:, j]
    outgoing, box_terms = lax.optimization_barrier((outgoing, box_terms))
    before_term = from_behind(box_terms[:, layers - 1].astype(jnp.bfloat16), "gz", 1)

    rate_full = jnp.broadcast_to(decay_rate, outgoing.shape)
    entering = entering_sums(outgoing, rate_full, float(layers))

    shifted = shift_layers(
        offsets, box_terms, entering, before_term, decay_rate, wave_x, wave_y, columns
    ).reshape(2, layers * plane_size, half_rows)
    local_out = None
    for part in range(2):
        product = lax.dot_general(
            x2l[:, part * half_rows : (part + 1) * half_rows],
            shifted[part],
            (((1,), (1,)), ((), ())),
            preferred_element_type=jnp.float32,
        )
        local_out = product if local_out is None else local_out + product
    return local_out.astype(jnp.bfloat16).reshape(coeffs, layers, plane_size)


def solution(mesh):
    in_specs = (P(None, "gz", "xy"), P("gz", "xy"), P(), P(), P(), P(), P(), P())
    out_specs = P(None, "gz", "xy")
    return jax.shard_map(body, mesh=mesh, in_specs=in_specs, out_specs=out_specs, check_vma=False)
```

```python
import jax
import jax.numpy as jnp
from jax import lax
from jax.experimental import pallas as pl
from jax.experimental.pallas import tpu as pltpu
from jax.sharding import PartitionSpec as P

BY = 8
R = 2
NOFF = 6
TILE_ROWS = 8
TILE = TILE_ROWS * 512


def from_behind(value, axis, steps):
    count = lax.axis_size(axis)
    pairs = [(source, (source + steps) % count) for source in range(count)]
    return lax.ppermute(value, axis, pairs)


def with_halo(block, axis, dim, width):
    low = from_behind(lax.slice_in_dim(block, block.shape[dim] - width, None, axis=dim), axis, 1)
    high = from_behind(lax.slice_in_dim(block, 0, width, axis=dim), axis, -1)
    return jnp.concatenate([low, block, high], axis=dim)


def cyclic_decayed_sum(held, gain_of):
    count = held.shape[0]
    result, offset, span, block, left = None, 0, 1, held, count
    while left:
        if left & 1:
            term = jnp.roll(block, offset, axis=0)
            if offset:
                term = gain_of(offset) * term
            result = term if result is None else result + term
            offset += span
        left >>= 1
        if left:
            block = block + gain_of(span) * jnp.roll(block, span, axis=0)
            span *= 2
    return result


def entering_sums(outgoing, rate_full, layers):
    shape = outgoing.shape
    size = outgoing.size
    count = lax.axis_size("gz")
    me = lax.axis_index("gz")
    chunk = -(-size // (count * TILE)) * TILE
    padded = chunk * count

    def spread(values, fill):
        flat = jnp.pad(values.reshape(-1), (0, padded - size), constant_values=fill)
        return flat.reshape(count, TILE_ROWS, chunk // TILE_ROWS)

    held = lax.all_to_all(spread(outgoing, 0.0), "gz", 0, 0, tiled=True)
    held = held.reshape(count, chunk)
    my_rates = lax.dynamic_index_in_dim(spread(rate_full, 1.0).reshape(count, chunk), me, 0, False)
    sums = cyclic_decayed_sum(held, lambda steps: jnp.exp(-my_rates * (layers * steps)))
    sums = jnp.roll(sums, 1, axis=0) / (1.0 - jnp.exp(-my_rates * (layers * count)))
    sums = sums.reshape(count, TILE_ROWS, chunk // TILE_ROWS)
    back = lax.all_to_all(sums, "gz", 0, 0, tiled=True)
    return back.reshape(-1)[:size].reshape(shape)


def shift_kernel(steps_ref, terms_ref, entering_ref, before_ref, factor_ref, cos_ref, sin_ref,
                 real_ref, imag_ref, field_ref):
    _, layers, boxes, width = terms_ref.shape
    _, columns, rows, _ = real_ref.shape
    factor = factor_ref[...]
    state = entering_ref[...]
    prev_term = before_ref[...].astype(jnp.float32)
    for i in range(layers):
        up = factor * (state - prev_term)
        fresh = terms_ref[:, i]
        state = factor * state + fresh
        prev_term = fresh
        up = up.astype(jnp.bfloat16).astype(jnp.float32)
        field_ref[...] = up.reshape(2, boxes // rows, rows, width)
        acc_real = jnp.zeros((columns, rows, width), jnp.float32)
        acc_imag = jnp.zeros((columns, rows, width), jnp.float32)
        for entry in range(NOFF):
            start = jnp.clip(R - steps_ref[entry, 0], 0, 2 * R)
            turn = lax.rem(steps_ref[entry, 1] + rows, rows)
            moved = field_ref[:, pl.ds(start, columns), :, :]
            moved = pltpu.roll(moved, turn, 2)
            cosine = cos_ref[entry]
            sine_part = sin_ref[entry]
            acc_real = acc_real + moved[0] * cosine - moved[1] * sine_part
            acc_imag = acc_imag + moved[0] * sine_part + moved[1] * cosine
        real_ref[i] = acc_real.astype(real_ref.dtype)
        imag_ref[i] = acc_imag.astype(imag_ref.dtype)


def shift_layers(offsets, box_terms, entering, before_term, rate, wave_x, wave_y, columns):
    _, layers, boxes, width = box_terms.shape
    factor = jnp.exp(-rate)[None, :]
    steps = offsets.astype(jnp.float32)
    phase_angle = steps[:, :1] * wave_x[None] + steps[:, 1:] * wave_y[None]
    vmem = pl.BlockSpec(memory_space=pltpu.VMEM)
    smem = pl.BlockSpec(memory_space=pltpu.SMEM)
    half = jax.ShapeDtypeStruct((layers, columns, BY, width), jnp.bfloat16)
    return pl.pallas_call(
        shift_kernel,
        out_shape=(half, half),
        in_specs=[smem] + [vmem] * 6,
        out_specs=(vmem, vmem),
        scratch_shapes=[pltpu.VMEM((2, boxes // BY, BY, width), jnp.float32)],
        cost_estimate=pl.CostEstimate(
            flops=2 * layers * boxes * width * 30,
            transcendentals=0,
            bytes_accessed=box_terms.size * 4 + 3 * entering.size * 4,
        ),
    )(offsets, box_terms, entering, before_term, factor,
      jnp.cos(phase_angle)[:, None, :], jnp.sin(phase_angle)[:, None, :])


def body(moments, counts, m2x, x2l, decay_rate, wave_x, wave_y, offsets):
    coeffs, layers, plane_size = moments.shape
    exp_rows = m2x.shape[0]
    half_rows = exp_rows // 2
    columns = plane_size // BY
    ext_columns = columns + 2 * R
    ext_boxes = ext_columns * BY
    rate = decay_rate[None, None, None, :]
    factor = jnp.exp(-rate)
    weight = jnp.sqrt(1.0 - factor * factor)
    multipole = (moments.astype(jnp.float32) * counts.astype(jnp.float32)[None]).astype(
        jnp.bfloat16
    )
    multipole = with_halo(multipole, "xy", 2, R * BY).reshape(coeffs, layers * ext_boxes)
    halves = []
    for part in range(2):
        rows = m2x[part * half_rows : (part + 1) * half_rows]
        expansion = lax.dot_general(
            multipole, rows, (((0,), (1,)), ((), ())), preferred_element_type=jnp.float32
        )
        halves.append(expansion.reshape(layers, ext_boxes, half_rows))
    box_terms = weight * jnp.stack(halves)

    outgoing = box_terms[:, layers - 1]
    for j in range(layers - 1):
        outgoing = outgoing + jnp.exp(-rate[0] * float(layers - 1 - j)) * box_terms[:, j]
    outgoing, box_terms = lax.optimization_barrier((outgoing, box_terms))
    before_term = from_behind(box_terms[:, layers - 1].astype(jnp.bfloat16), "gz", 1)

    rate_full = jnp.broadcast_to(decay_rate, outgoing.shape)
    entering = entering_sums(outgoing, rate_full, float(layers))

    shifted = shift_layers(
        offsets, box_terms, entering, before_term, decay_rate, wave_x, wave_y, columns
    )
    local_out = None
    for part in range(2):
        product = lax.dot_general(
            x2l[:, part * half_rows : (part + 1) * half_rows],
            shifted[part].reshape(layers * plane_size, half_rows),
            (((1,), (1,)), ((), ())),
            preferred_element_type=jnp.float32,
        )
        local_out = product if local_out is None else local_out + product
    return local_out.astype(jnp.bfloat16).reshape(coeffs, layers, plane_size)


def solution(mesh):
    in_specs = (P(None, "gz", "xy"), P("gz", "xy"), P(), P(), P(), P(), P(), P())
    out_specs = P(None, "gz", "xy")
    return jax.shard_map(body, mesh=mesh, in_specs=in_specs, out_specs=out_specs, check_vma=False)
```

```python
import jax
import jax.numpy as jnp
from jax import lax
from jax.experimental import pallas as pl
from jax.experimental.pallas import tpu as pltpu
from jax.sharding import PartitionSpec as P

BY = 8
R = 2
NOFF = 6
TILE_ROWS = 8
TILE = TILE_ROWS * 512


def from_behind(value, axis, steps):
    count = lax.axis_size(axis)
    pairs = [(source, (source + steps) % count) for source in range(count)]
    return lax.ppermute(value, axis, pairs)


def with_halo(block, axis, dim, width):
    low = from_behind(lax.slice_in_dim(block, block.shape[dim] - width, None, axis=dim), axis, 1)
    high = from_behind(lax.slice_in_dim(block, 0, width, axis=dim), axis, -1)
    return jnp.concatenate([low, block, high], axis=dim)


def cyclic_decayed_sum(held, gain_of):
    count = held.shape[0]
    result, offset, span, block, left = None, 0, 1, held, count
    while left:
        if left & 1:
            term = jnp.roll(block, offset, axis=0)
            if offset:
                term = gain_of(offset) * term
            result = term if result is None else result + term
            offset += span
        left >>= 1
        if left:
            block = block + gain_of(span) * jnp.roll(block, span, axis=0)
            span *= 2
    return result


def entering_sums(outgoing, rate_full, layers):
    shape = outgoing.shape
    size = outgoing.size
    count = lax.axis_size("gz")
    me = lax.axis_index("gz")
    chunk = -(-size // (count * TILE)) * TILE
    padded = chunk * count

    def spread(values, fill):
        flat = jnp.pad(values.reshape(-1), (0, padded - size), constant_values=fill)
        return flat.reshape(count, TILE_ROWS, chunk // TILE_ROWS)

    held = lax.all_to_all(spread(outgoing, 0.0), "gz", 0, 0, tiled=True)
    held = held.reshape(count, chunk)
    my_rates = lax.dynamic_index_in_dim(spread(rate_full, 1.0).reshape(count, chunk), me, 0, False)
    sums = cyclic_decayed_sum(held, lambda steps: jnp.exp(-my_rates * (layers * steps)))
    sums = jnp.roll(sums, 1, axis=0) / (1.0 - jnp.exp(-my_rates * (layers * count)))
    sums = sums.reshape(count, TILE_ROWS, chunk // TILE_ROWS)
    back = lax.all_to_all(sums, "gz", 0, 0, tiled=True)
    return back.reshape(-1)[:size].reshape(shape)


def shift_kernel(steps_ref, terms_ref, entering_ref, before_ref, factor_ref, cos_ref, sin_ref,
                 real_ref, imag_ref, field_ref):
    _, layers, boxes, width = terms_ref.shape
    _, columns, rows, _ = real_ref.shape
    factor = factor_ref[...]
    state = entering_ref[...]
    prev_term = before_ref[...].astype(jnp.float32)
    starts = [jnp.clip(R - steps_ref[entry, 0], 0, 2 * R) for entry in range(NOFF)]
    turns = [lax.rem(steps_ref[entry, 1] + rows, rows) for entry in range(NOFF)]
    for i in range(layers):
        up = factor * (state - prev_term)
        fresh = terms_ref[:, i]
        state = factor * state + fresh
        prev_term = fresh
        up = up.astype(jnp.bfloat16).astype(jnp.float32)
        field_ref[...] = up.reshape(2, boxes // rows, rows, width)

        def column(x, carry, i=i):
            acc_real = jnp.zeros((rows, width), jnp.float32)
            acc_imag = jnp.zeros((rows, width), jnp.float32)
            for entry in range(NOFF):
                moved = field_ref[:, starts[entry] + x, :, :]
                moved = pltpu.roll(moved, turns[entry], 1)
                cosine = cos_ref[entry]
                sine_part = sin_ref[entry]
                acc_real = acc_real + moved[0] * cosine - moved[1] * sine_part
                acc_imag = acc_imag + moved[0] * sine_part + moved[1] * cosine
            real_ref[i, x] = acc_real.astype(real_ref.dtype)
            imag_ref[i, x] = acc_imag.astype(imag_ref.dtype)
            return carry

        lax.fori_loop(0, columns, column, 0)


def shift_layers(offsets, box_terms, entering, before_term, rate, wave_x, wave_y, columns):
    _, layers, boxes, width = box_terms.shape
    factor = jnp.exp(-rate)[None, :]
    steps = offsets.astype(jnp.float32)
    phase_angle = steps[:, :1] * wave_x[None] + steps[:, 1:] * wave_y[None]
    vmem = pl.BlockSpec(memory_space=pltpu.VMEM)
    smem = pl.BlockSpec(memory_space=pltpu.SMEM)
    half = jax.ShapeDtypeStruct((layers, columns, BY, width), jnp.bfloat16)
    return pl.pallas_call(
        shift_kernel,
        out_shape=(half, half),
        in_specs=[smem] + [vmem] * 6,
        out_specs=(vmem, vmem),
        scratch_shapes=[pltpu.VMEM((2, boxes // BY, BY, width), jnp.float32)],
        cost_estimate=pl.CostEstimate(
            flops=2 * layers * boxes * width * 30,
            transcendentals=0,
            bytes_accessed=box_terms.size * 4 + 3 * entering.size * 4,
        ),
    )(offsets, box_terms, entering, before_term, factor,
      jnp.cos(phase_angle)[:, None, :], jnp.sin(phase_angle)[:, None, :])


def body(moments, counts, m2x, x2l, decay_rate, wave_x, wave_y, offsets):
    coeffs, layers, plane_size = moments.shape
    exp_rows = m2x.shape[0]
    half_rows = exp_rows // 2
    columns = plane_size // BY
    ext_columns = columns + 2 * R
    ext_boxes = ext_columns * BY
    rate = decay_rate[None, None, None, :]
    factor = jnp.exp(-rate)
    weight = jnp.sqrt(1.0 - factor * factor)
    multipole = (moments.astype(jnp.float32) * counts.astype(jnp.float32)[None]).astype(
        jnp.bfloat16
    )
    multipole = with_halo(multipole, "xy", 2, R * BY).reshape(coeffs, layers * ext_boxes)
    halves = []
    for part in range(2):
        rows = m2x[part * half_rows : (part + 1) * half_rows]
        expansion = lax.dot_general(
            multipole, rows, (((0,), (1,)), ((), ())), preferred_element_type=jnp.float32
        )
        halves.append(expansion.reshape(layers, ext_boxes, half_rows))
    box_terms = weight * jnp.stack(halves)

    outgoing = box_terms[:, layers - 1]
    for j in range(layers - 1):
        outgoing = outgoing + jnp.exp(-rate[0] * float(layers - 1 - j)) * box_terms[:, j]
    outgoing, box_terms = lax.optimization_barrier((outgoing, box_terms))
    before_term = from_behind(box_terms[:, layers - 1].astype(jnp.bfloat16), "gz", 1)

    rate_full = jnp.broadcast_to(decay_rate, outgoing.shape)
    entering = entering_sums(outgoing, rate_full, float(layers))

    shifted = shift_layers(
        offsets, box_terms, entering, before_term, decay_rate, wave_x, wave_y, columns
    )
    local_out = None
    for part in range(2):
        product = lax.dot_general(
            x2l[:, part * half_rows : (part + 1) * half_rows],
            shifted[part].reshape(layers * plane_size, half_rows),
            (((1,), (1,)), ((), ())),
            preferred_element_type=jnp.float32,
        )
        local_out = product if local_out is None else local_out + product
    return local_out.astype(jnp.bfloat16).reshape(coeffs, layers, plane_size)


def solution(mesh):
    in_specs = (P(None, "gz", "xy"), P("gz", "xy"), P(), P(), P(), P(), P(), P())
    out_specs = P(None, "gz", "xy")
    return jax.shard_map(body, mesh=mesh, in_specs=in_specs, out_specs=out_specs, check_vma=False)
```

```python
import jax
import jax.numpy as jnp
from jax import lax
from jax.experimental import pallas as pl
from jax.experimental.pallas import tpu as pltpu
from jax.sharding import PartitionSpec as P

BY = 8
R = 2
NOFF = 6
TILE_ROWS = 8
TILE = TILE_ROWS * 512


def from_behind(value, axis, steps):
    count = lax.axis_size(axis)
    pairs = [(source, (source + steps) % count) for source in range(count)]
    return lax.ppermute(value, axis, pairs)


def with_halo(block, axis, dim, width):
    low = from_behind(lax.slice_in_dim(block, block.shape[dim] - width, None, axis=dim), axis, 1)
    high = from_behind(lax.slice_in_dim(block, 0, width, axis=dim), axis, -1)
    return jnp.concatenate([low, block, high], axis=dim)


def cyclic_decayed_sum(held, gain_of):
    count = held.shape[0]
    result, offset, span, block, left = None, 0, 1, held, count
    while left:
        if left & 1:
            term = jnp.roll(block, offset, axis=0)
            if offset:
                term = gain_of(offset) * term
            result = term if result is None else result + term
            offset += span
        left >>= 1
        if left:
            block = block + gain_of(span) * jnp.roll(block, span, axis=0)
            span *= 2
    return result


def entering_sums(outgoing, rate_full, layers):
    shape = outgoing.shape
    size = outgoing.size
    count = lax.axis_size("gz")
    me = lax.axis_index("gz")
    chunk = -(-size // (count * TILE)) * TILE
    padded = chunk * count

    def spread(values, fill):
        flat = jnp.pad(values.reshape(-1), (0, padded - size), constant_values=fill)
        return flat.reshape(count, TILE_ROWS, chunk // TILE_ROWS)

    held = lax.all_to_all(spread(outgoing, 0.0), "gz", 0, 0, tiled=True)
    held = held.reshape(count, chunk)
    my_rates = lax.dynamic_index_in_dim(spread(rate_full, 1.0).reshape(count, chunk), me, 0, False)
    sums = cyclic_decayed_sum(held, lambda steps: jnp.exp(-my_rates * (layers * steps)))
    sums = jnp.roll(sums, 1, axis=0) / (1.0 - jnp.exp(-my_rates * (layers * count)))
    sums = sums.reshape(count, TILE_ROWS, chunk // TILE_ROWS)
    back = lax.all_to_all(sums, "gz", 0, 0, tiled=True)
    return back.reshape(-1)[:size].reshape(shape)


def shift_kernel(steps_ref, terms_ref, entering_ref, before_ref, factor_ref, cos_ref, sin_ref,
                 real_ref, imag_ref, field_ref):
    _, layers, boxes, width = terms_ref.shape
    _, columns, rows, _ = real_ref.shape
    factor = factor_ref[...]
    state = entering_ref[...]
    prev_term = before_ref[...].astype(jnp.float32)
    starts = [jnp.clip(R - steps_ref[entry, 0], 0, 2 * R) for entry in range(NOFF)]
    turns = [lax.rem(steps_ref[entry, 1] + rows, rows) for entry in range(NOFF)]
    for i in range(layers):
        up = factor * (state - prev_term)
        fresh = terms_ref[:, i]
        state = factor * state + fresh
        prev_term = fresh
        up = up.astype(jnp.bfloat16).astype(jnp.float32)
        field_ref[...] = up.reshape(2, boxes // rows, rows, width)

        def column(x, carry, i=i):
            acc_real = jnp.zeros((rows, width), jnp.float32)
            acc_imag = jnp.zeros((rows, width), jnp.float32)
            for entry in range(NOFF):
                moved = field_ref[:, starts[entry] + x, :, :]
                moved = pltpu.roll(moved, turns[entry], 1)
                cosine = cos_ref[entry]
                sine_part = sin_ref[entry]
                acc_real = acc_real + moved[0] * cosine - moved[1] * sine_part
                acc_imag = acc_imag + moved[0] * sine_part + moved[1] * cosine
            real_ref[i, x] = acc_real.astype(real_ref.dtype)
            imag_ref[i, x] = acc_imag.astype(imag_ref.dtype)
            return carry

        lax.fori_loop(0, columns, column, 0)


def shift_layers(offsets, box_terms, entering, before_term, rate, wave_x, wave_y, columns):
    _, layers, boxes, width = box_terms.shape
    factor = jnp.exp(-rate)[None, :]
    steps = offsets.astype(jnp.float32)
    phase_angle = steps[:, :1] * wave_x[None] + steps[:, 1:] * wave_y[None]
    vmem = pl.BlockSpec(memory_space=pltpu.VMEM)
    smem = pl.BlockSpec(memory_space=pltpu.SMEM)
    half = jax.ShapeDtypeStruct((layers, columns, BY, width), jnp.bfloat16)
    return pl.pallas_call(
        shift_kernel,
        out_shape=(half, half),
        in_specs=[smem] + [vmem] * 6,
        out_specs=(vmem, vmem),
        scratch_shapes=[pltpu.VMEM((2, boxes // BY, BY, width), jnp.float32)],
        cost_estimate=pl.CostEstimate(
            flops=2 * layers * boxes * width * 30,
            transcendentals=0,
            bytes_accessed=box_terms.size * 4 + 3 * entering.size * 4,
        ),
    )(offsets, box_terms, entering, before_term, factor,
      jnp.cos(phase_angle)[:, None, :], jnp.sin(phase_angle)[:, None, :])


def body(moments, counts, m2x, x2l, decay_rate, wave_x, wave_y, offsets):
    coeffs, layers, plane_size = moments.shape
    exp_rows = m2x.shape[0]
    half_rows = exp_rows // 2
    columns = plane_size // BY
    ext_columns = columns + 2 * R
    ext_boxes = ext_columns * BY
    rate = decay_rate[None, None, None, :]
    factor = jnp.exp(-rate)
    weight = jnp.sqrt(1.0 - factor * factor)
    multipole = (moments.astype(jnp.float32) * counts.astype(jnp.float32)[None]).astype(
        jnp.bfloat16
    )
    multipole = with_halo(multipole, "xy", 2, R * BY).reshape(coeffs, layers * ext_boxes)
    halves = []
    for part in range(2):
        rows = m2x[part * half_rows : (part + 1) * half_rows]
        expansion = lax.dot_general(
            multipole, rows, (((0,), (1,)), ((), ())), preferred_element_type=jnp.float32
        )
        halves.append(expansion.reshape(layers, ext_boxes, half_rows))
    box_terms = weight * jnp.stack(halves)

    outgoing = box_terms[:, layers - 1]
    for j in range(layers - 1):
        outgoing = outgoing + jnp.exp(-rate[0] * float(layers - 1 - j)) * box_terms[:, j]
    before_term = from_behind(box_terms[:, layers - 1].astype(jnp.bfloat16), "gz", 1)

    rate_full = jnp.broadcast_to(decay_rate, outgoing.shape)
    entering = entering_sums(outgoing, rate_full, float(layers))

    shifted = shift_layers(
        offsets, box_terms, entering, before_term, decay_rate, wave_x, wave_y, columns
    )
    local_out = None
    for part in range(2):
        product = lax.dot_general(
            x2l[:, part * half_rows : (part + 1) * half_rows],
            shifted[part].reshape(layers * plane_size, half_rows),
            (((1,), (1,)), ((), ())),
            preferred_element_type=jnp.float32,
        )
        local_out = product if local_out is None else local_out + product
    return local_out.astype(jnp.bfloat16).reshape(coeffs, layers, plane_size)


def solution(mesh):
    in_specs = (P(None, "gz", "xy"), P("gz", "xy"), P(), P(), P(), P(), P(), P())
    out_specs = P(None, "gz", "xy")
    return jax.shard_map(body, mesh=mesh, in_specs=in_specs, out_specs=out_specs, check_vma=False)
```

```python
import jax
import jax.numpy as jnp
from jax import lax
from jax.experimental import pallas as pl
from jax.experimental.pallas import tpu as pltpu
from jax.sharding import PartitionSpec as P

BY = 8
R = 2
NOFF = 6
TILE_ROWS = 8
TILE = TILE_ROWS * 512


def from_behind(value, axis, steps):
    count = lax.axis_size(axis)
    pairs = [(source, (source + steps) % count) for source in range(count)]
    return lax.ppermute(value, axis, pairs)


def with_halo(block, axis, dim, width):
    low = from_behind(lax.slice_in_dim(block, block.shape[dim] - width, None, axis=dim), axis, 1)
    high = from_behind(lax.slice_in_dim(block, 0, width, axis=dim), axis, -1)
    return jnp.concatenate([low, block, high], axis=dim)


def cyclic_decayed_sum(held, gain_of):
    count = held.shape[0]
    result, offset, span, block, left = None, 0, 1, held, count
    while left:
        if left & 1:
            term = jnp.roll(block, offset, axis=0)
            if offset:
                term = gain_of(offset) * term
            result = term if result is None else result + term
            offset += span
        left >>= 1
        if left:
            block = block + gain_of(span) * jnp.roll(block, span, axis=0)
            span *= 2
    return result


def entering_sums(outgoing, rate_full, layers):
    shape = outgoing.shape
    size = outgoing.size
    count = lax.axis_size("gz")
    me = lax.axis_index("gz")
    chunk = -(-size // (count * TILE)) * TILE
    padded = chunk * count

    def spread(values, fill):
        flat = jnp.pad(values.reshape(-1), (0, padded - size), constant_values=fill)
        return flat.reshape(count, TILE_ROWS, chunk // TILE_ROWS)

    held = lax.all_to_all(spread(outgoing, 0.0), "gz", 0, 0, tiled=True)
    held = held.reshape(count, chunk)
    my_rates = lax.dynamic_index_in_dim(spread(rate_full, 1.0).reshape(count, chunk), me, 0, False)
    sums = cyclic_decayed_sum(held, lambda steps: jnp.exp(-my_rates * (layers * steps)))
    sums = jnp.roll(sums, 1, axis=0) / (1.0 - jnp.exp(-my_rates * (layers * count)))
    sums = sums.reshape(count, TILE_ROWS, chunk // TILE_ROWS)
    back = lax.all_to_all(sums, "gz", 0, 0, tiled=True)
    return back.reshape(-1)[:size].reshape(shape)


def shift_kernel(steps_ref, terms_ref, entering_ref, before_ref, factor_ref, cos_ref, sin_ref,
                 real_ref, imag_ref, field_ref):
    _, layers, ext_columns, rows, width = terms_ref.shape
    _, columns, _, _ = real_ref.shape
    factor = factor_ref[...]
    starts = [jnp.clip(R - steps_ref[entry, 0], 0, 2 * R) for entry in range(NOFF)]
    turns = [lax.rem(steps_ref[entry, 1] + rows, rows) for entry in range(NOFF)]

    def build(c, carry):
        state = entering_ref[:, c]
        prev_term = before_ref[:, c].astype(jnp.float32)
        for i in range(layers):
            up = factor * (state - prev_term)
            fresh = terms_ref[:, i, c]
            state = factor * state + fresh
            prev_term = fresh
            field_ref[i, :, c] = up.astype(jnp.bfloat16).astype(jnp.float32)
        return carry

    lax.fori_loop(0, ext_columns, build, 0)
    for i in range(layers):

        def column(x, carry, i=i):
            acc_real = jnp.zeros((rows, width), jnp.float32)
            acc_imag = jnp.zeros((rows, width), jnp.float32)
            for entry in range(NOFF):
                moved = field_ref[i, :, starts[entry] + x, :, :]
                moved = pltpu.roll(moved, turns[entry], 1)
                cosine = cos_ref[entry]
                sine_part = sin_ref[entry]
                acc_real = acc_real + moved[0] * cosine - moved[1] * sine_part
                acc_imag = acc_imag + moved[0] * sine_part + moved[1] * cosine
            real_ref[i, x] = acc_real.astype(real_ref.dtype)
            imag_ref[i, x] = acc_imag.astype(imag_ref.dtype)
            return carry

        lax.fori_loop(0, columns, column, 0)


def shift_layers(offsets, box_terms, entering, before_term, rate, wave_x, wave_y, columns):
    _, layers, boxes, width = box_terms.shape
    factor = jnp.exp(-rate)[None, :]
    steps = offsets.astype(jnp.float32)
    phase_angle = steps[:, :1] * wave_x[None] + steps[:, 1:] * wave_y[None]
    vmem = pl.BlockSpec(memory_space=pltpu.VMEM)
    smem = pl.BlockSpec(memory_space=pltpu.SMEM)
    half = jax.ShapeDtypeStruct((layers, columns, BY, width), jnp.bfloat16)
    return pl.pallas_call(
        shift_kernel,
        out_shape=(half, half),
        in_specs=[smem] + [vmem] * 6,
        out_specs=(vmem, vmem),
        scratch_shapes=[pltpu.VMEM((layers, 2, boxes // BY, BY, width), jnp.float32)],
        cost_estimate=pl.CostEstimate(
            flops=2 * layers * boxes * width * 30,
            transcendentals=0,
            bytes_accessed=box_terms.size * 4 + 3 * entering.size * 4,
        ),
    )(offsets, box_terms.reshape(2, layers, boxes // BY, BY, width),
      entering.reshape(2, boxes // BY, BY, width), before_term.reshape(2, boxes // BY, BY, width), factor,
      jnp.cos(phase_angle)[:, None, :], jnp.sin(phase_angle)[:, None, :])


def body(moments, counts, m2x, x2l, decay_rate, wave_x, wave_y, offsets):
    coeffs, layers, plane_size = moments.shape
    exp_rows = m2x.shape[0]
    half_rows = exp_rows // 2
    columns = plane_size // BY
    ext_columns = columns + 2 * R
    ext_boxes = ext_columns * BY
    rate = decay_rate[None, None, None, :]
    factor = jnp.exp(-rate)
    weight = jnp.sqrt(1.0 - factor * factor)
    multipole = (moments.astype(jnp.float32) * counts.astype(jnp.float32)[None]).astype(
        jnp.bfloat16
    )
    multipole = with_halo(multipole, "xy", 2, R * BY).reshape(coeffs, layers * ext_boxes)
    halves = []
    for part in range(2):
        rows = m2x[part * half_rows : (part + 1) * half_rows]
        expansion = lax.dot_general(
            multipole, rows, (((0,), (1,)), ((), ())), preferred_element_type=jnp.float32
        )
        halves.append(expansion.reshape(layers, ext_boxes, half_rows))
    box_terms = weight * jnp.stack(halves)

    outgoing = box_terms[:, layers - 1]
    for j in range(layers - 1):
        outgoing = outgoing + jnp.exp(-rate[0] * float(layers - 1 - j)) * box_terms[:, j]
    outgoing, box_terms = lax.optimization_barrier((outgoing, box_terms))
    before_term = from_behind(box_terms[:, layers - 1].astype(jnp.bfloat16), "gz", 1)

    rate_full = jnp.broadcast_to(decay_rate, outgoing.shape)
    entering = entering_sums(outgoing, rate_full, float(layers))

    shifted = shift_layers(
        offsets, box_terms, entering, before_term, decay_rate, wave_x, wave_y, columns
    )
    local_out = None
    for part in range(2):
        product = lax.dot_general(
            x2l[:, part * half_rows : (part + 1) * half_rows],
            shifted[part].reshape(layers * plane_size, half_rows),
            (((1,), (1,)), ((), ())),
            preferred_element_type=jnp.float32,
        )
        local_out = product if local_out is None else local_out + product
    return local_out.astype(jnp.bfloat16).reshape(coeffs, layers, plane_size)


def solution(mesh):
    in_specs = (P(None, "gz", "xy"), P("gz", "xy"), P(), P(), P(), P(), P(), P())
    out_specs = P(None, "gz", "xy")
    return jax.shard_map(body, mesh=mesh, in_specs=in_specs, out_specs=out_specs, check_vma=False)
```

```python
import jax
import jax.numpy as jnp
from jax import lax
from jax.experimental import pallas as pl
from jax.experimental.pallas import tpu as pltpu
from jax.sharding import PartitionSpec as P

BY = 8
R = 2
NOFF = 6
TILE_ROWS = 8
TILE = TILE_ROWS * 512


def from_behind(value, axis, steps):
    count = lax.axis_size(axis)
    pairs = [(source, (source + steps) % count) for source in range(count)]
    return lax.ppermute(value, axis, pairs)


def with_halo(block, axis, dim, width):
    low = from_behind(lax.slice_in_dim(block, block.shape[dim] - width, None, axis=dim), axis, 1)
    high = from_behind(lax.slice_in_dim(block, 0, width, axis=dim), axis, -1)
    return jnp.concatenate([low, block, high], axis=dim)


def cyclic_decayed_sum(held, gain_of):
    count = held.shape[0]
    result, offset, span, block, left = None, 0, 1, held, count
    while left:
        if left & 1:
            term = jnp.roll(block, offset, axis=0)
            if offset:
                term = gain_of(offset) * term
            result = term if result is None else result + term
            offset += span
        left >>= 1
        if left:
            block = block + gain_of(span) * jnp.roll(block, span, axis=0)
            span *= 2
    return result


def entering_sums(outgoing, rate_full, layers):
    shape = outgoing.shape
    size = outgoing.size
    count = lax.axis_size("gz")
    me = lax.axis_index("gz")
    chunk = -(-size // (count * TILE)) * TILE
    padded = chunk * count

    def spread(values, fill):
        flat = jnp.pad(values.reshape(-1), (0, padded - size), constant_values=fill)
        return flat.reshape(count, TILE_ROWS, chunk // TILE_ROWS)

    held = lax.all_to_all(spread(outgoing, 0.0), "gz", 0, 0, tiled=True)
    held = held.reshape(count, chunk)
    my_rates = lax.dynamic_index_in_dim(spread(rate_full, 1.0).reshape(count, chunk), me, 0, False)
    sums = cyclic_decayed_sum(held, lambda steps: jnp.exp(-my_rates * (layers * steps)))
    sums = jnp.roll(sums, 1, axis=0) / (1.0 - jnp.exp(-my_rates * (layers * count)))
    sums = sums.reshape(count, TILE_ROWS, chunk // TILE_ROWS)
    back = lax.all_to_all(sums, "gz", 0, 0, tiled=True)
    return back.reshape(-1)[:size].reshape(shape)


def shift_kernel(steps_ref, terms_ref, entering_ref, before_ref, factor_ref, cos_ref, sin_ref,
                 real_ref, imag_ref, field_ref):
    _, layers, ext_columns, rows, width = terms_ref.shape
    _, columns, _, _ = real_ref.shape
    factor = factor_ref[...]
    starts = [jnp.clip(R - steps_ref[entry, 0], 0, 2 * R) for entry in range(NOFF)]
    turns = [lax.rem(steps_ref[entry, 1] + rows, rows) for entry in range(NOFF)]

    def build(c, carry):
        state = entering_ref[:, c]
        prev_term = before_ref[:, c].astype(jnp.float32)
        for i in range(layers):
            up = factor * (state - prev_term)
            fresh = terms_ref[:, i, c]
            state = factor * state + fresh
            prev_term = fresh
            field_ref[i, :, c] = up.astype(jnp.bfloat16).astype(jnp.float32)
        return carry

    lax.fori_loop(0, ext_columns, build, 0)
    for i in range(layers):

        def column(x, carry, i=i):
            acc_real = jnp.zeros((rows, width), jnp.float32)
            acc_imag = jnp.zeros((rows, width), jnp.float32)
            for entry in range(NOFF):
                moved = field_ref[i, :, starts[entry] + x, :, :]
                moved = pltpu.roll(moved, turns[entry], 1)
                cosine = cos_ref[entry]
                sine_part = sin_ref[entry]
                acc_real = acc_real + moved[0] * cosine - moved[1] * sine_part
                acc_imag = acc_imag + moved[0] * sine_part + moved[1] * cosine
            real_ref[i, x] = acc_real.astype(real_ref.dtype)
            imag_ref[i, x] = acc_imag.astype(imag_ref.dtype)
            return carry

        lax.fori_loop(0, columns, column, 0, unroll=2)


def shift_layers(offsets, box_terms, entering, before_term, rate, wave_x, wave_y, columns):
    _, layers, boxes, width = box_terms.shape
    factor = jnp.exp(-rate)[None, :]
    steps = offsets.astype(jnp.float32)
    phase_angle = steps[:, :1] * wave_x[None] + steps[:, 1:] * wave_y[None]
    vmem = pl.BlockSpec(memory_space=pltpu.VMEM)
    smem = pl.BlockSpec(memory_space=pltpu.SMEM)
    half = jax.ShapeDtypeStruct((layers, columns, BY, width), jnp.bfloat16)
    return pl.pallas_call(
        shift_kernel,
        out_shape=(half, half),
        in_specs=[smem] + [vmem] * 6,
        out_specs=(vmem, vmem),
        scratch_shapes=[pltpu.VMEM((layers, 2, boxes // BY, BY, width), jnp.float32)],
        cost_estimate=pl.CostEstimate(
            flops=2 * layers * boxes * width * 30,
            transcendentals=0,
            bytes_accessed=box_terms.size * 4 + 3 * entering.size * 4,
        ),
    )(offsets, box_terms.reshape(2, layers, boxes // BY, BY, width),
      entering.reshape(2, boxes // BY, BY, width), before_term.reshape(2, boxes // BY, BY, width), factor,
      jnp.broadcast_to(jnp.cos(phase_angle)[:, None, :], (NOFF, BY, width)),
      jnp.broadcast_to(jnp.sin(phase_angle)[:, None, :], (NOFF, BY, width)))


def body(moments, counts, m2x, x2l, decay_rate, wave_x, wave_y, offsets):
    coeffs, layers, plane_size = moments.shape
    exp_rows = m2x.shape[0]
    half_rows = exp_rows // 2
    columns = plane_size // BY
    ext_columns = columns + 2 * R
    ext_boxes = ext_columns * BY
    rate = decay_rate[None, None, None, :]
    factor = jnp.exp(-rate)
    weight = jnp.sqrt(1.0 - factor * factor)
    multipole = (moments.astype(jnp.float32) * counts.astype(jnp.float32)[None]).astype(
        jnp.bfloat16
    )
    multipole = with_halo(multipole, "xy", 2, R * BY).reshape(coeffs, layers * ext_boxes)
    halves = []
    for part in range(2):
        rows = m2x[part * half_rows : (part + 1) * half_rows]
        expansion = lax.dot_general(
            multipole, rows, (((0,), (1,)), ((), ())), preferred_element_type=jnp.float32
        )
        halves.append(expansion.reshape(layers, ext_boxes, half_rows))
    box_terms = weight * jnp.stack(halves)

    outgoing = box_terms[:, layers - 1]
    for j in range(layers - 1):
        outgoing = outgoing + jnp.exp(-rate[0] * float(layers - 1 - j)) * box_terms[:, j]
    outgoing, box_terms = lax.optimization_barrier((outgoing, box_terms))
    before_term = from_behind(box_terms[:, layers - 1].astype(jnp.bfloat16), "gz", 1)

    rate_full = jnp.broadcast_to(decay_rate, outgoing.shape)
    entering = entering_sums(outgoing, rate_full, float(layers))

    shifted = shift_layers(
        offsets, box_terms, entering, before_term, decay_rate, wave_x, wave_y, columns
    )
    local_out = None
    for part in range(2):
        product = lax.dot_general(
            x2l[:, part * half_rows : (part + 1) * half_rows],
            shifted[part].reshape(layers * plane_size, half_rows),
            (((1,), (1,)), ((), ())),
            preferred_element_type=jnp.float32,
        )
        local_out = product if local_out is None else local_out + product
    return local_out.astype(jnp.bfloat16).reshape(coeffs, layers, plane_size)


def solution(mesh):
    in_specs = (P(None, "gz", "xy"), P("gz", "xy"), P(), P(), P(), P(), P(), P())
    out_specs = P(None, "gz", "xy")
    return jax.shard_map(body, mesh=mesh, in_specs=in_specs, out_specs=out_specs, check_vma=False)
```

```python
import jax
import jax.numpy as jnp
from jax import lax
from jax.experimental import pallas as pl
from jax.experimental.pallas import tpu as pltpu
from jax.sharding import PartitionSpec as P

BY = 8
R = 2
NOFF = 6
TILE_ROWS = 8
TILE = TILE_ROWS * 512


def from_behind(value, axis, steps):
    count = lax.axis_size(axis)
    pairs = [(source, (source + steps) % count) for source in range(count)]
    return lax.ppermute(value, axis, pairs)


def with_halo(block, axis, dim, width):
    tail = lax.slice_in_dim(block, block.shape[dim] - width, None, axis=dim)
    head = lax.slice_in_dim(block, 0, width, axis=dim)
    if lax.axis_size(axis) == 2:
        both = from_behind(jnp.concatenate([tail, head], axis=dim), axis, 1)
        low = lax.slice_in_dim(both, 0, width, axis=dim)
        high = lax.slice_in_dim(both, width, None, axis=dim)
    else:
        low = from_behind(tail, axis, 1)
        high = from_behind(head, axis, -1)
    return jnp.concatenate([low, block, high], axis=dim)


def cyclic_decayed_sum(held, gain_of):
    count = held.shape[0]
    result, offset, span, block, left = None, 0, 1, held, count
    while left:
        if left & 1:
            term = jnp.roll(block, offset, axis=0)
            if offset:
                term = gain_of(offset) * term
            result = term if result is None else result + term
            offset += span
        left >>= 1
        if left:
            block = block + gain_of(span) * jnp.roll(block, span, axis=0)
            span *= 2
    return result


def entering_sums(outgoing, rate_full, layers):
    shape = outgoing.shape
    size = outgoing.size
    count = lax.axis_size("gz")
    me = lax.axis_index("gz")
    chunk = -(-size // (count * TILE)) * TILE
    padded = chunk * count

    def spread(values, fill):
        flat = jnp.pad(values.reshape(-1), (0, padded - size), constant_values=fill)
        return flat.reshape(count, TILE_ROWS, chunk // TILE_ROWS)

    held = lax.all_to_all(spread(outgoing, 0.0), "gz", 0, 0, tiled=True)
    held = held.reshape(count, chunk)
    my_rates = lax.dynamic_index_in_dim(spread(rate_full, 1.0).reshape(count, chunk), me, 0, False)
    sums = cyclic_decayed_sum(held, lambda steps: jnp.exp(-my_rates * (layers * steps)))
    sums = jnp.roll(sums, 1, axis=0) / (1.0 - jnp.exp(-my_rates * (layers * count)))
    sums = sums.reshape(count, TILE_ROWS, chunk // TILE_ROWS)
    back = lax.all_to_all(sums, "gz", 0, 0, tiled=True)
    return back.reshape(-1)[:size].reshape(shape)


def shift_kernel(steps_ref, terms_ref, entering_ref, before_ref, factor_ref, cos_ref, sin_ref,
                 real_ref, imag_ref, field_ref):
    _, layers, ext_columns, rows, width = terms_ref.shape
    _, columns, _, _ = real_ref.shape
    factor = factor_ref[...]
    starts = [jnp.clip(R - steps_ref[entry, 0], 0, 2 * R) for entry in range(NOFF)]
    turns = [lax.rem(steps_ref[entry, 1] + rows, rows) for entry in range(NOFF)]

    def build(c, carry):
        state = entering_ref[:, c]
        prev_term = before_ref[:, c].astype(jnp.float32)
        for i in range(layers):
            up = factor * (state - prev_term)
            fresh = terms_ref[:, i, c]
            state = factor * state + fresh
            prev_term = fresh
            field_ref[i, :, c] = up.astype(jnp.bfloat16).astype(jnp.float32)
        return carry

    lax.fori_loop(0, ext_columns, build, 0)
    for i in range(layers):

        def column(x, carry, i=i):
            acc_real = jnp.zeros((rows, width), jnp.float32)
            acc_imag = jnp.zeros((rows, width), jnp.float32)
            for entry in range(NOFF):
                moved = field_ref[i, :, starts[entry] + x, :, :]
                moved = pltpu.roll(moved, turns[entry], 1)
                cosine = cos_ref[entry]
                sine_part = sin_ref[entry]
                acc_real = acc_real + moved[0] * cosine - moved[1] * sine_part
                acc_imag = acc_imag + moved[0] * sine_part + moved[1] * cosine
            real_ref[i, x] = acc_real.astype(real_ref.dtype)
            imag_ref[i, x] = acc_imag.astype(imag_ref.dtype)
            return carry

        lax.fori_loop(0, columns, column, 0, unroll=2)


def shift_layers(offsets, box_terms, entering, before_term, rate, wave_x, wave_y, columns):
    _, layers, boxes, width = box_terms.shape
    factor = jnp.exp(-rate)[None, :]
    steps = offsets.astype(jnp.float32)
    phase_angle = steps[:, :1] * wave_x[None] + steps[:, 1:] * wave_y[None]
    vmem = pl.BlockSpec(memory_space=pltpu.VMEM)
    smem = pl.BlockSpec(memory_space=pltpu.SMEM)
    half = jax.ShapeDtypeStruct((layers, columns, BY, width), jnp.bfloat16)
    return pl.pallas_call(
        shift_kernel,
        out_shape=(half, half),
        in_specs=[smem] + [vmem] * 6,
        out_specs=(vmem, vmem),
        scratch_shapes=[pltpu.VMEM((layers, 2, boxes // BY, BY, width), jnp.float32)],
        cost_estimate=pl.CostEstimate(
            flops=2 * layers * boxes * width * 30,
            transcendentals=0,
            bytes_accessed=box_terms.size * 4 + 3 * entering.size * 4,
        ),
    )(offsets, box_terms.reshape(2, layers, boxes // BY, BY, width),
      entering.reshape(2, boxes // BY, BY, width), before_term.reshape(2, boxes // BY, BY, width), factor,
      jnp.broadcast_to(jnp.cos(phase_angle)[:, None, :], (NOFF, BY, width)),
      jnp.broadcast_to(jnp.sin(phase_angle)[:, None, :], (NOFF, BY, width)))


def body(moments, counts, m2x, x2l, decay_rate, wave_x, wave_y, offsets):
    coeffs, layers, plane_size = moments.shape
    exp_rows = m2x.shape[0]
    half_rows = exp_rows // 2
    columns = plane_size // BY
    ext_columns = columns + 2 * R
    ext_boxes = ext_columns * BY
    rate = decay_rate[None, None, None, :]
    factor = jnp.exp(-rate)
    weight = jnp.sqrt(1.0 - factor * factor)
    multipole = (moments.astype(jnp.float32) * counts.astype(jnp.float32)[None]).astype(
        jnp.bfloat16
    )
    multipole = with_halo(multipole, "xy", 2, R * BY).reshape(coeffs, layers * ext_boxes)
    halves = []
    for part in range(2):
        rows = m2x[part * half_rows : (part + 1) * half_rows]
        expansion = lax.dot_general(
            multipole, rows, (((0,), (1,)), ((), ())), preferred_element_type=jnp.float32
        )
        halves.append(expansion.reshape(layers, ext_boxes, half_rows))
    box_terms = weight * jnp.stack(halves)

    outgoing = box_terms[:, layers - 1]
    for j in range(layers - 1):
        outgoing = outgoing + jnp.exp(-rate[0] * float(layers - 1 - j)) * box_terms[:, j]
    outgoing, box_terms = lax.optimization_barrier((outgoing, box_terms))
    before_term = from_behind(box_terms[:, layers - 1].astype(jnp.bfloat16), "gz", 1)

    rate_full = jnp.broadcast_to(decay_rate, outgoing.shape)
    entering = entering_sums(outgoing, rate_full, float(layers))

    shifted = shift_layers(
        offsets, box_terms, entering, before_term, decay_rate, wave_x, wave_y, columns
    )
    local_out = None
    for part in range(2):
        product = lax.dot_general(
            x2l[:, part * half_rows : (part + 1) * half_rows],
            shifted[part].reshape(layers * plane_size, half_rows),
            (((1,), (1,)), ((), ())),
            preferred_element_type=jnp.float32,
        )
        local_out = product if local_out is None else local_out + product
    return local_out.astype(jnp.bfloat16).reshape(coeffs, layers, plane_size)


def solution(mesh):
    in_specs = (P(None, "gz", "xy"), P("gz", "xy"), P(), P(), P(), P(), P(), P())
    out_specs = P(None, "gz", "xy")
    return jax.shard_map(body, mesh=mesh, in_specs=in_specs, out_specs=out_specs, check_vma=False)
```

```python
import jax
import jax.numpy as jnp
from jax import lax
from jax.experimental import pallas as pl
from jax.experimental.pallas import tpu as pltpu
from jax.sharding import PartitionSpec as P

BY = 8
R = 2
NOFF = 6
TILE_ROWS = 8
TILE = TILE_ROWS * 512


def from_behind(value, axis, steps):
    count = lax.axis_size(axis)
    pairs = [(source, (source + steps) % count) for source in range(count)]
    return lax.ppermute(value, axis, pairs)


def with_halo(block, axis, dim, width):
    tail = lax.slice_in_dim(block, block.shape[dim] - width, None, axis=dim)
    head = lax.slice_in_dim(block, 0, width, axis=dim)
    if lax.axis_size(axis) == 2:
        both = from_behind(jnp.concatenate([tail, head], axis=dim), axis, 1)
        low = lax.slice_in_dim(both, 0, width, axis=dim)
        high = lax.slice_in_dim(both, width, None, axis=dim)
    else:
        low = from_behind(tail, axis, 1)
        high = from_behind(head, axis, -1)
    return jnp.concatenate([low, block, high], axis=dim)


def cyclic_decayed_sum(held, gain_of):
    count = held.shape[0]
    result, offset, span, block, left = None, 0, 1, held, count
    while left:
        if left & 1:
            term = jnp.roll(block, offset, axis=0)
            if offset:
                term = gain_of(offset) * term
            result = term if result is None else result + term
            offset += span
        left >>= 1
        if left:
            block = block + gain_of(span) * jnp.roll(block, span, axis=0)
            span *= 2
    return result


def entering_sums(outgoing, rate_full, layers):
    shape = outgoing.shape
    size = outgoing.size
    count = lax.axis_size("gz")
    me = lax.axis_index("gz")
    chunk = -(-size // (count * TILE)) * TILE
    padded = chunk * count

    def spread(values, fill):
        flat = jnp.pad(values.reshape(-1), (0, padded - size), constant_values=fill)
        return flat.reshape(count, TILE_ROWS, chunk // TILE_ROWS)

    held = lax.all_to_all(spread(outgoing, 0.0), "gz", 0, 0, tiled=True)
    held = held.reshape(count, chunk)
    my_rates = lax.dynamic_index_in_dim(spread(rate_full, 1.0).reshape(count, chunk), me, 0, False)
    sums = cyclic_decayed_sum(held, lambda steps: jnp.exp(-my_rates * (layers * steps)))
    sums = jnp.roll(sums, 1, axis=0) / (1.0 - jnp.exp(-my_rates * (layers * count)))
    sums = sums.reshape(count, TILE_ROWS, chunk // TILE_ROWS)
    back = lax.all_to_all(sums, "gz", 0, 0, tiled=True)
    return back.reshape(-1)[:size].reshape(shape)


def shift_kernel(steps_ref, terms_ref, entering_ref, before_ref, factor_ref, cos_ref, sin_ref,
                 real_ref, imag_ref, field_ref):
    _, layers, ext_columns, rows, width = terms_ref.shape
    _, columns, _, _ = real_ref.shape
    factor = factor_ref[...]
    starts = [jnp.clip(R - steps_ref[entry, 0], 0, 2 * R) for entry in range(NOFF)]
    turns = [lax.rem(steps_ref[entry, 1] + rows, rows) for entry in range(NOFF)]

    def build(c, carry):
        state = entering_ref[:, c]
        prev_term = before_ref[:, c].astype(jnp.float32)
        for i in range(layers):
            up = factor * (state - prev_term)
            fresh = terms_ref[:, i, c]
            state = factor * state + fresh
            prev_term = fresh
            field_ref[i, :, c] = up.astype(jnp.bfloat16).astype(jnp.float32)
        return carry

    lax.fori_loop(0, ext_columns, build, 0)
    for i in range(layers):

        def column(x, carry, i=i):
            acc_real = jnp.zeros((rows, width), jnp.float32)
            acc_imag = jnp.zeros((rows, width), jnp.float32)
            for entry in range(NOFF):
                moved = field_ref[i, :, starts[entry] + x, :, :]
                moved = pltpu.roll(moved, turns[entry], 1)
                cosine = cos_ref[entry]
                sine_part = sin_ref[entry]
                acc_real = acc_real + moved[0] * cosine - moved[1] * sine_part
                acc_imag = acc_imag + moved[0] * sine_part + moved[1] * cosine
            real_ref[i, x] = acc_real.astype(real_ref.dtype)
            imag_ref[i, x] = acc_imag.astype(imag_ref.dtype)
            return carry

        lax.fori_loop(0, columns, column, 0, unroll=2)


def shift_layers(offsets, box_terms, entering, before_term, rate, wave_x, wave_y, columns):
    _, layers, boxes, width = box_terms.shape
    factor = jnp.exp(-rate)[None, :]
    steps = offsets.astype(jnp.float32)
    phase_angle = steps[:, :1] * wave_x[None] + steps[:, 1:] * wave_y[None]
    vmem = pl.BlockSpec(memory_space=pltpu.VMEM)
    smem = pl.BlockSpec(memory_space=pltpu.SMEM)
    half = jax.ShapeDtypeStruct((layers, columns, BY, width), jnp.bfloat16)
    return pl.pallas_call(
        shift_kernel,
        out_shape=(half, half),
        in_specs=[smem] + [vmem] * 6,
        out_specs=(vmem, vmem),
        scratch_shapes=[pltpu.VMEM((layers, 2, boxes // BY, BY, width), jnp.float32)],
        cost_estimate=pl.CostEstimate(
            flops=2 * layers * boxes * width * 30,
            transcendentals=0,
            bytes_accessed=box_terms.size * 4 + 3 * entering.size * 4,
        ),
    )(offsets, box_terms.reshape(2, layers, boxes // BY, BY, width),
      entering.reshape(2, boxes // BY, BY, width), before_term.reshape(2, boxes // BY, BY, width), factor,
      jnp.broadcast_to(jnp.cos(phase_angle)[:, None, :], (NOFF, BY, width)),
      jnp.broadcast_to(jnp.sin(phase_angle)[:, None, :], (NOFF, BY, width)))


def body(moments, counts, m2x, x2l, decay_rate, wave_x, wave_y, offsets):
    coeffs, layers, plane_size = moments.shape
    exp_rows = m2x.shape[0]
    half_rows = exp_rows // 2
    columns = plane_size // BY
    ext_columns = columns + 2 * R
    ext_boxes = ext_columns * BY
    rate = decay_rate[None, None, None, :]
    factor = jnp.exp(-rate)
    weight = jnp.sqrt(1.0 - factor * factor)
    multipole = (moments.astype(jnp.float32) * counts.astype(jnp.float32)[None]).astype(
        jnp.bfloat16
    )
    multipole = with_halo(multipole, "xy", 2, R * BY).reshape(coeffs, layers * ext_boxes)
    halves = []
    for part in range(2):
        rows = m2x[part * half_rows : (part + 1) * half_rows]
        expansion = lax.dot_general(
            multipole, rows, (((0,), (1,)), ((), ())), preferred_element_type=jnp.float32
        )
        halves.append(expansion.reshape(layers, ext_boxes, half_rows))
    box_terms = weight * jnp.stack(halves)

    outgoing = box_terms[:, layers - 1]
    for j in range(layers - 1):
        outgoing = outgoing + jnp.exp(-rate[0] * float(layers - 1 - j)) * box_terms[:, j]
    outgoing = lax.optimization_barrier(outgoing)
    before_term = from_behind(box_terms[:, layers - 1].astype(jnp.bfloat16), "gz", 1)

    rate_full = jnp.broadcast_to(decay_rate, outgoing.shape)
    entering = entering_sums(outgoing, rate_full, float(layers))

    shifted = shift_layers(
        offsets, box_terms, entering, before_term, decay_rate, wave_x, wave_y, columns
    )
    local_out = None
    for part in range(2):
        product = lax.dot_general(
            x2l[:, part * half_rows : (part + 1) * half_rows],
            shifted[part].reshape(layers * plane_size, half_rows),
            (((1,), (1,)), ((), ())),
            preferred_element_type=jnp.float32,
        )
        local_out = product if local_out is None else local_out + product
    return local_out.astype(jnp.bfloat16).reshape(coeffs, layers, plane_size)


def solution(mesh):
    in_specs = (P(None, "gz", "xy"), P("gz", "xy"), P(), P(), P(), P(), P(), P())
    out_specs = P(None, "gz", "xy")
    return jax.shard_map(body, mesh=mesh, in_specs=in_specs, out_specs=out_specs, check_vma=False)
```

```python
import jax
import jax.numpy as jnp
from jax import lax
from jax.experimental import pallas as pl
from jax.experimental.pallas import tpu as pltpu
from jax.sharding import PartitionSpec as P

BY = 8
R = 2
NOFF = 6
TILE_ROWS = 8
TILE = TILE_ROWS * 512


def from_behind(value, axis, steps):
    count = lax.axis_size(axis)
    pairs = [(source, (source + steps) % count) for source in range(count)]
    return lax.ppermute(value, axis, pairs)


def with_halo(block, axis, dim, width):
    tail = lax.slice_in_dim(block, block.shape[dim] - width, None, axis=dim)
    head = lax.slice_in_dim(block, 0, width, axis=dim)
    if lax.axis_size(axis) == 2:
        both = from_behind(jnp.concatenate([tail, head], axis=dim), axis, 1)
        low = lax.slice_in_dim(both, 0, width, axis=dim)
        high = lax.slice_in_dim(both, width, None, axis=dim)
    else:
        low = from_behind(tail, axis, 1)
        high = from_behind(head, axis, -1)
    return jnp.concatenate([low, block, high], axis=dim)


def cyclic_decayed_sum(held, gain_of):
    count = held.shape[0]
    result, offset, span, block, left = None, 0, 1, held, count
    while left:
        if left & 1:
            term = jnp.roll(block, offset, axis=0)
            if offset:
                term = gain_of(offset) * term
            result = term if result is None else result + term
            offset += span
        left >>= 1
        if left:
            block = block + gain_of(span) * jnp.roll(block, span, axis=0)
            span *= 2
    return result


def entering_sums(outgoing, rate_full, layers):
    shape = outgoing.shape
    size = outgoing.size
    count = lax.axis_size("gz")
    me = lax.axis_index("gz")
    chunk = -(-size // (count * TILE)) * TILE
    padded = chunk * count

    def spread(values, fill):
        flat = jnp.pad(values.reshape(-1), (0, padded - size), constant_values=fill)
        return flat.reshape(count, TILE_ROWS, chunk // TILE_ROWS)

    held = lax.all_to_all(spread(outgoing, 0.0), "gz", 0, 0, tiled=True)
    held = held.reshape(count, chunk)
    my_rates = lax.dynamic_index_in_dim(spread(rate_full, 1.0).reshape(count, chunk), me, 0, False)
    sums = cyclic_decayed_sum(held, lambda steps: jnp.exp(-my_rates * (layers * steps)))
    sums = jnp.roll(sums, 1, axis=0) / (1.0 - jnp.exp(-my_rates * (layers * count)))
    sums = sums.reshape(count, TILE_ROWS, chunk // TILE_ROWS)
    back = lax.all_to_all(sums, "gz", 0, 0, tiled=True)
    return back.reshape(-1)[:size].reshape(shape)


def shift_kernel(steps_ref, terms_ref, entering_ref, before_ref, factor_ref, cos_ref, sin_ref,
                 real_ref, imag_ref, field_ref):
    _, layers, ext_columns, rows, width = terms_ref.shape
    _, columns, _, _ = real_ref.shape
    factor = factor_ref[...]
    starts = [jnp.clip(R - steps_ref[entry, 0], 0, 2 * R) for entry in range(NOFF)]
    turns = [lax.rem(steps_ref[entry, 1] + rows, rows) for entry in range(NOFF)]

    def build(c, carry):
        state = entering_ref[:, c]
        prev_term = before_ref[:, c].astype(jnp.float32)
        for i in range(layers):
            up = factor * (state - prev_term)
            fresh = terms_ref[:, i, c]
            state = factor * state + fresh
            prev_term = fresh
            field_ref[i, :, c] = up.astype(jnp.bfloat16).astype(jnp.float32)
        return carry

    lax.fori_loop(0, ext_columns, build, 0)
    for i in range(layers):

        def column(x, carry, i=i):
            acc_real = jnp.zeros((rows, width), jnp.float32)
            acc_imag = jnp.zeros((rows, width), jnp.float32)
            for entry in range(NOFF):
                moved = field_ref[i, :, starts[entry] + x, :, :]
                moved = pltpu.roll(moved, turns[entry], 1)
                cosine = cos_ref[entry]
                sine_part = sin_ref[entry]
                acc_real = acc_real + moved[0] * cosine - moved[1] * sine_part
                acc_imag = acc_imag + moved[0] * sine_part + moved[1] * cosine
            real_ref[i, x] = acc_real.astype(real_ref.dtype)
            imag_ref[i, x] = acc_imag.astype(imag_ref.dtype)
            return carry

        lax.fori_loop(0, columns, column, 0, unroll=4)


def shift_layers(offsets, box_terms, entering, before_term, rate, wave_x, wave_y, columns):
    _, layers, boxes, width = box_terms.shape
    factor = jnp.exp(-rate)[None, :]
    steps = offsets.astype(jnp.float32)
    phase_angle = steps[:, :1] * wave_x[None] + steps[:, 1:] * wave_y[None]
    vmem = pl.BlockSpec(memory_space=pltpu.VMEM)
    smem = pl.BlockSpec(memory_space=pltpu.SMEM)
    half = jax.ShapeDtypeStruct((layers, columns, BY, width), jnp.bfloat16)
    return pl.pallas_call(
        shift_kernel,
        out_shape=(half, half),
        in_specs=[smem] + [vmem] * 6,
        out_specs=(vmem, vmem),
        scratch_shapes=[pltpu.VMEM((layers, 2, boxes // BY, BY, width), jnp.float32)],
        cost_estimate=pl.CostEstimate(
            flops=2 * layers * boxes * width * 30,
            transcendentals=0,
            bytes_accessed=box_terms.size * 4 + 3 * entering.size * 4,
        ),
    )(offsets, box_terms.reshape(2, layers, boxes // BY, BY, width),
      entering.reshape(2, boxes // BY, BY, width), before_term.reshape(2, boxes // BY, BY, width), factor,
      jnp.broadcast_to(jnp.cos(phase_angle)[:, None, :], (NOFF, BY, width)),
      jnp.broadcast_to(jnp.sin(phase_angle)[:, None, :], (NOFF, BY, width)))


def body(moments, counts, m2x, x2l, decay_rate, wave_x, wave_y, offsets):
    coeffs, layers, plane_size = moments.shape
    exp_rows = m2x.shape[0]
    half_rows = exp_rows // 2
    columns = plane_size // BY
    ext_columns = columns + 2 * R
    ext_boxes = ext_columns * BY
    rate = decay_rate[None, None, None, :]
    factor = jnp.exp(-rate)
    weight = jnp.sqrt(1.0 - factor * factor)
    multipole = (moments.astype(jnp.float32) * counts.astype(jnp.float32)[None]).astype(
        jnp.bfloat16
    )
    multipole = with_halo(multipole, "xy", 2, R * BY).reshape(coeffs, layers * ext_boxes)
    halves = []
    for part in range(2):
        rows = m2x[part * half_rows : (part + 1) * half_rows]
        expansion = lax.dot_general(
            multipole, rows, (((0,), (1,)), ((), ())), preferred_element_type=jnp.float32
        )
        halves.append(expansion.reshape(layers, ext_boxes, half_rows))
    box_terms = weight * jnp.stack(halves)

    outgoing = box_terms[:, layers - 1]
    for j in range(layers - 1):
        outgoing = outgoing + jnp.exp(-rate[0] * float(layers - 1 - j)) * box_terms[:, j]
    outgoing, box_terms = lax.optimization_barrier((outgoing, box_terms))
    before_term = from_behind(box_terms[:, layers - 1].astype(jnp.bfloat16), "gz", 1)

    rate_full = jnp.broadcast_to(decay_rate, outgoing.shape)
    entering = entering_sums(outgoing, rate_full, float(layers))

    shifted = shift_layers(
        offsets, box_terms, entering, before_term, decay_rate, wave_x, wave_y, columns
    )
    local_out = None
    for part in range(2):
        product = lax.dot_general(
            x2l[:, part * half_rows : (part + 1) * half_rows],
            shifted[part].reshape(layers * plane_size, half_rows),
            (((1,), (1,)), ((), ())),
            preferred_element_type=jnp.float32,
        )
        local_out = product if local_out is None else local_out + product
    return local_out.astype(jnp.bfloat16).reshape(coeffs, layers, plane_size)


def solution(mesh):
    in_specs = (P(None, "gz", "xy"), P("gz", "xy"), P(), P(), P(), P(), P(), P())
    out_specs = P(None, "gz", "xy")
    return jax.shard_map(body, mesh=mesh, in_specs=in_specs, out_specs=out_specs, check_vma=False)
```

```python
import jax
import jax.numpy as jnp
from jax import lax
from jax.experimental import pallas as pl
from jax.experimental.pallas import tpu as pltpu
from jax.sharding import PartitionSpec as P

BY = 8
R = 2
NOFF = 6
TILE_ROWS = 8
TILE = TILE_ROWS * 512


def from_behind(value, axis, steps):
    count = lax.axis_size(axis)
    pairs = [(source, (source + steps) % count) for source in range(count)]
    return lax.ppermute(value, axis, pairs)


def with_halo(block, axis, dim, width):
    tail = lax.slice_in_dim(block, block.shape[dim] - width, None, axis=dim)
    head = lax.slice_in_dim(block, 0, width, axis=dim)
    if lax.axis_size(axis) == 2:
        both = from_behind(jnp.concatenate([tail, head], axis=dim), axis, 1)
        low = lax.slice_in_dim(both, 0, width, axis=dim)
        high = lax.slice_in_dim(both, width, None, axis=dim)
    else:
        low = from_behind(tail, axis, 1)
        high = from_behind(head, axis, -1)
    return jnp.concatenate([low, block, high], axis=dim)


def cyclic_decayed_sum(held, gain_of):
    count = held.shape[0]
    result, offset, span, block, left = None, 0, 1, held, count
    while left:
        if left & 1:
            term = jnp.roll(block, offset, axis=0)
            if offset:
                term = gain_of(offset) * term
            result = term if result is None else result + term
            offset += span
        left >>= 1
        if left:
            block = block + gain_of(span) * jnp.roll(block, span, axis=0)
            span *= 2
    return result


def entering_sums(outgoing, rate_full, layers):
    shape = outgoing.shape
    size = outgoing.size
    count = lax.axis_size("gz")
    me = lax.axis_index("gz")
    chunk = -(-size // (count * TILE)) * TILE
    padded = chunk * count

    def spread(values, fill):
        flat = jnp.pad(values.reshape(-1), (0, padded - size), constant_values=fill)
        return flat.reshape(count, TILE_ROWS, chunk // TILE_ROWS)

    held = lax.all_to_all(spread(outgoing, 0.0), "gz", 0, 0, tiled=True)
    held = held.reshape(count, chunk)
    my_rates = lax.dynamic_index_in_dim(spread(rate_full, 1.0).reshape(count, chunk), me, 0, False)
    sums = cyclic_decayed_sum(held, lambda steps: jnp.exp(-my_rates * (layers * steps)))
    sums = jnp.roll(sums, 1, axis=0) / (1.0 - jnp.exp(-my_rates * (layers * count)))
    sums = sums.reshape(count, TILE_ROWS, chunk // TILE_ROWS)
    back = lax.all_to_all(sums, "gz", 0, 0, tiled=True)
    return back.reshape(-1)[:size].reshape(shape)


def shift_kernel(steps_ref, terms_ref, entering_ref, before_ref, factor_ref, cos_ref, sin_ref,
                 real_ref, imag_ref, field_ref):
    _, layers, ext_columns, rows, width = terms_ref.shape
    _, columns, _, _ = real_ref.shape
    factor = factor_ref[...]
    starts = [jnp.clip(R - steps_ref[entry, 0], 0, 2 * R) for entry in range(NOFF)]
    turns = [lax.rem(steps_ref[entry, 1] + rows, rows) for entry in range(NOFF)]

    def build(c, carry):
        state = entering_ref[:, c]
        prev_term = before_ref[:, c].astype(jnp.float32)
        for i in range(layers):
            up = factor * (state - prev_term)
            fresh = terms_ref[:, i, c]
            state = factor * state + fresh
            prev_term = fresh
            field_ref[i, :, c] = up.astype(jnp.bfloat16).astype(jnp.float32)
        return carry

    lax.fori_loop(0, ext_columns, build, 0)
    for i in range(layers):

        def column(x, carry, i=i):
            acc_real = jnp.zeros((rows, width), jnp.float32)
            acc_imag = jnp.zeros((rows, width), jnp.float32)
            for entry in range(NOFF):
                moved = field_ref[i, :, starts[entry] + x, :, :]
                moved = pltpu.roll(moved, turns[entry], 1)
                cosine = cos_ref[entry]
                sine_part = sin_ref[entry]
                acc_real = acc_real + moved[0] * cosine - moved[1] * sine_part
                acc_imag = acc_imag + moved[0] * sine_part + moved[1] * cosine
            real_ref[i, x] = acc_real.astype(real_ref.dtype)
            imag_ref[i, x] = acc_imag.astype(imag_ref.dtype)
            return carry

        lax.fori_loop(0, columns, column, 0, unroll=8)


def shift_layers(offsets, box_terms, entering, before_term, rate, wave_x, wave_y, columns):
    _, layers, boxes, width = box_terms.shape
    factor = jnp.exp(-rate)[None, :]
    steps = offsets.astype(jnp.float32)
    phase_angle = steps[:, :1] * wave_x[None] + steps[:, 1:] * wave_y[None]
    vmem = pl.BlockSpec(memory_space=pltpu.VMEM)
    smem = pl.BlockSpec(memory_space=pltpu.SMEM)
    half = jax.ShapeDtypeStruct((layers, columns, BY, width), jnp.bfloat16)
    return pl.pallas_call(
        shift_kernel,
        out_shape=(half, half),
        in_specs=[smem] + [vmem] * 6,
        out_specs=(vmem, vmem),
        scratch_shapes=[pltpu.VMEM((layers, 2, boxes // BY, BY, width), jnp.float32)],
        cost_estimate=pl.CostEstimate(
            flops=2 * layers * boxes * width * 30,
            transcendentals=0,
            bytes_accessed=box_terms.size * 4 + 3 * entering.size * 4,
        ),
    )(offsets, box_terms.reshape(2, layers, boxes // BY, BY, width),
      entering.reshape(2, boxes // BY, BY, width), before_term.reshape(2, boxes // BY, BY, width), factor,
      jnp.broadcast_to(jnp.cos(phase_angle)[:, None, :], (NOFF, BY, width)),
      jnp.broadcast_to(jnp.sin(phase_angle)[:, None, :], (NOFF, BY, width)))


def body(moments, counts, m2x, x2l, decay_rate, wave_x, wave_y, offsets):
    coeffs, layers, plane_size = moments.shape
    exp_rows = m2x.shape[0]
    half_rows = exp_rows // 2
    columns = plane_size // BY
    ext_columns = columns + 2 * R
    ext_boxes = ext_columns * BY
    rate = decay_rate[None, None, None, :]
    factor = jnp.exp(-rate)
    weight = jnp.sqrt(1.0 - factor * factor)
    multipole = (moments.astype(jnp.float32) * counts.astype(jnp.float32)[None]).astype(
        jnp.bfloat16
    )
    multipole = with_halo(multipole, "xy", 2, R * BY).reshape(coeffs, layers * ext_boxes)
    halves = []
    for part in range(2):
        rows = m2x[part * half_rows : (part + 1) * half_rows]
        expansion = lax.dot_general(
            multipole, rows, (((0,), (1,)), ((), ())), preferred_element_type=jnp.float32
        )
        halves.append(expansion.reshape(layers, ext_boxes, half_rows))
    box_terms = weight * jnp.stack(halves)

    outgoing = box_terms[:, layers - 1]
    for j in range(layers - 1):
        outgoing = outgoing + jnp.exp(-rate[0] * float(layers - 1 - j)) * box_terms[:, j]
    outgoing, box_terms = lax.optimization_barrier((outgoing, box_terms))
    before_term = from_behind(box_terms[:, layers - 1].astype(jnp.bfloat16), "gz", 1)

    rate_full = jnp.broadcast_to(decay_rate, outgoing.shape)
    entering = entering_sums(outgoing, rate_full, float(layers))

    shifted = shift_layers(
        offsets, box_terms, entering, before_term, decay_rate, wave_x, wave_y, columns
    )
    local_out = None
    for part in range(2):
        product = lax.dot_general(
            x2l[:, part * half_rows : (part + 1) * half_rows],
            shifted[part].reshape(layers * plane_size, half_rows),
            (((1,), (1,)), ((), ())),
            preferred_element_type=jnp.float32,
        )
        local_out = product if local_out is None else local_out + product
    return local_out.astype(jnp.bfloat16).reshape(coeffs, layers, plane_size)


def solution(mesh):
    in_specs = (P(None, "gz", "xy"), P("gz", "xy"), P(), P(), P(), P(), P(), P())
    out_specs = P(None, "gz", "xy")
    return jax.shard_map(body, mesh=mesh, in_specs=in_specs, out_specs=out_specs, check_vma=False)
```

```python
import jax
import jax.numpy as jnp
from jax import lax
from jax.experimental import pallas as pl
from jax.experimental.pallas import tpu as pltpu
from jax.sharding import PartitionSpec as P

BY = 8
R = 2
NOFF = 6
TILE_ROWS = 8
TILE = TILE_ROWS * 512


def from_behind(value, axis, steps):
    count = lax.axis_size(axis)
    pairs = [(source, (source + steps) % count) for source in range(count)]
    return lax.ppermute(value, axis, pairs)


def with_halo(block, axis, dim, width):
    tail = lax.slice_in_dim(block, block.shape[dim] - width, None, axis=dim)
    head = lax.slice_in_dim(block, 0, width, axis=dim)
    if lax.axis_size(axis) == 2:
        both = from_behind(jnp.concatenate([tail, head], axis=dim), axis, 1)
        low = lax.slice_in_dim(both, 0, width, axis=dim)
        high = lax.slice_in_dim(both, width, None, axis=dim)
    else:
        low = from_behind(tail, axis, 1)
        high = from_behind(head, axis, -1)
    return jnp.concatenate([low, block, high], axis=dim)


def cyclic_decayed_sum(held, gain_of):
    count = held.shape[0]
    result, offset, span, block, left = None, 0, 1, held, count
    while left:
        if left & 1:
            term = jnp.roll(block, offset, axis=0)
            if offset:
                term = gain_of(offset) * term
            result = term if result is None else result + term
            offset += span
        left >>= 1
        if left:
            block = block + gain_of(span) * jnp.roll(block, span, axis=0)
            span *= 2
    return result


def entering_sums(outgoing, rate_full, layers):
    shape = outgoing.shape
    size = outgoing.size
    count = lax.axis_size("gz")
    me = lax.axis_index("gz")
    chunk = -(-size // (count * TILE)) * TILE
    padded = chunk * count

    def spread(values, fill):
        flat = jnp.pad(values.reshape(-1), (0, padded - size), constant_values=fill)
        return flat.reshape(count, TILE_ROWS, chunk // TILE_ROWS)

    held = lax.all_to_all(spread(outgoing, 0.0), "gz", 0, 0, tiled=True)
    held = held.reshape(count, chunk)
    my_rates = lax.dynamic_index_in_dim(spread(rate_full, 1.0).reshape(count, chunk), me, 0, False)
    sums = cyclic_decayed_sum(held, lambda steps: jnp.exp(-my_rates * (layers * steps)))
    sums = jnp.roll(sums, 1, axis=0) / (1.0 - jnp.exp(-my_rates * (layers * count)))
    sums = sums.reshape(count, TILE_ROWS, chunk // TILE_ROWS)
    back = lax.all_to_all(sums, "gz", 0, 0, tiled=True)
    return back.reshape(-1)[:size].reshape(shape)


def shift_kernel(steps_ref, terms_ref, entering_ref, before_ref, factor_ref, cos_ref, sin_ref,
                 real_ref, imag_ref, field_ref):
    _, layers, ext_columns, rows, width = terms_ref.shape
    _, columns, _, _ = real_ref.shape
    factor = factor_ref[...]
    starts = [jnp.clip(R - steps_ref[entry, 0], 0, 2 * R) for entry in range(NOFF)]
    turns = [lax.rem(steps_ref[entry, 1] + rows, rows) for entry in range(NOFF)]

    def build(c, carry):
        state = entering_ref[:, c]
        prev_term = before_ref[:, c].astype(jnp.float32)
        for i in range(layers):
            up = factor * (state - prev_term)
            fresh = terms_ref[:, i, c]
            state = factor * state + fresh
            prev_term = fresh
            field_ref[i, :, c] = up.astype(jnp.bfloat16).astype(jnp.float32)
        return carry

    lax.fori_loop(0, ext_columns, build, 0)
    for i in range(layers):

        def column(x, carry, i=i):
            acc_real = jnp.zeros((rows, width), jnp.float32)
            acc_imag = jnp.zeros((rows, width), jnp.float32)
            for entry in range(NOFF):
                moved = field_ref[i, :, starts[entry] + x, :, :]
                moved = pltpu.roll(moved, turns[entry], 1)
                cosine = cos_ref[entry]
                sine_part = sin_ref[entry]
                acc_real = acc_real + moved[0] * cosine - moved[1] * sine_part
                acc_imag = acc_imag + moved[0] * sine_part + moved[1] * cosine
            real_ref[i, x] = acc_real.astype(real_ref.dtype)
            imag_ref[i, x] = acc_imag.astype(imag_ref.dtype)
            return carry

        lax.fori_loop(0, columns, column, 0, unroll=4)


def shift_layers(offsets, box_terms, entering, before_term, rate, wave_x, wave_y, columns):
    _, layers, boxes, width = box_terms.shape
    factor = jnp.exp(-rate)[None, :]
    steps = offsets.astype(jnp.float32)
    phase_angle = steps[:, :1] * wave_x[None] + steps[:, 1:] * wave_y[None]
    vmem = pl.BlockSpec(memory_space=pltpu.VMEM)
    smem = pl.BlockSpec(memory_space=pltpu.SMEM)
    half = jax.ShapeDtypeStruct((layers, columns, BY, width), jnp.bfloat16)
    return pl.pallas_call(
        shift_kernel,
        out_shape=(half, half),
        in_specs=[smem] + [vmem] * 6,
        out_specs=(vmem, vmem),
        scratch_shapes=[pltpu.VMEM((layers, 2, boxes // BY, BY, width), jnp.float32)],
        cost_estimate=pl.CostEstimate(
            flops=2 * layers * boxes * width * 30,
            transcendentals=0,
            bytes_accessed=box_terms.size * 4 + 3 * entering.size * 4,
        ),
    )(offsets, box_terms.reshape(2, layers, boxes // BY, BY, width),
      entering.reshape(2, boxes // BY, BY, width), before_term.reshape(2, boxes // BY, BY, width), factor,
      jnp.broadcast_to(jnp.cos(phase_angle)[:, None, :], (NOFF, BY, width)),
      jnp.broadcast_to(jnp.sin(phase_angle)[:, None, :], (NOFF, BY, width)))


def body(moments, counts, m2x, x2l, decay_rate, wave_x, wave_y, offsets):
    coeffs, layers, plane_size = moments.shape
    exp_rows = m2x.shape[0]
    half_rows = exp_rows // 2
    columns = plane_size // BY
    ext_columns = columns + 2 * R
    ext_boxes = ext_columns * BY
    rate = decay_rate[None, None, None, :]
    factor = jnp.exp(-rate)
    weight = jnp.sqrt(1.0 - factor * factor)
    multipole = (moments.astype(jnp.float32) * counts.astype(jnp.float32)[None]).astype(
        jnp.bfloat16
    )
    multipole = with_halo(multipole, "xy", 2, R * BY).reshape(coeffs, layers * ext_boxes)
    halves = []
    for part in range(2):
        rows = m2x[part * half_rows : (part + 1) * half_rows]
        expansion = lax.dot_general(
            multipole, rows, (((0,), (1,)), ((), ())), preferred_element_type=jnp.float32
        )
        halves.append(expansion.reshape(layers, ext_boxes, half_rows))
    box_terms = weight * jnp.stack(halves)

    outgoing = box_terms[:, layers - 1]
    for j in range(layers - 1):
        outgoing = outgoing + jnp.exp(-rate[0] * float(layers - 1 - j)) * box_terms[:, j]
    before_term = from_behind(box_terms[:, layers - 1].astype(jnp.bfloat16), "gz", 1)
    outgoing, box_terms, before_term = lax.optimization_barrier((outgoing, box_terms, before_term))

    rate_full = jnp.broadcast_to(decay_rate, outgoing.shape)
    entering = entering_sums(outgoing, rate_full, float(layers))

    shifted = shift_layers(
        offsets, box_terms, entering, before_term, decay_rate, wave_x, wave_y, columns
    )
    local_out = None
    for part in range(2):
        product = lax.dot_general(
            x2l[:, part * half_rows : (part + 1) * half_rows],
            shifted[part].reshape(layers * plane_size, half_rows),
            (((1,), (1,)), ((), ())),
            preferred_element_type=jnp.float32,
        )
        local_out = product if local_out is None else local_out + product
    return local_out.astype(jnp.bfloat16).reshape(coeffs, layers, plane_size)


def solution(mesh):
    in_specs = (P(None, "gz", "xy"), P("gz", "xy"), P(), P(), P(), P(), P(), P())
    out_specs = P(None, "gz", "xy")
    return jax.shard_map(body, mesh=mesh, in_specs=in_specs, out_specs=out_specs, check_vma=False)
```

```python
import jax
import jax.numpy as jnp
from jax import lax
from jax.experimental import pallas as pl
from jax.experimental.pallas import tpu as pltpu
from jax.sharding import PartitionSpec as P

BY = 8
R = 2
NOFF = 6
TILE_ROWS = 8
TILE = TILE_ROWS * 512


def from_behind(value, axis, steps):
    count = lax.axis_size(axis)
    pairs = [(source, (source + steps) % count) for source in range(count)]
    return lax.ppermute(value, axis, pairs)


def with_halo(block, axis, dim, width):
    tail = lax.slice_in_dim(block, block.shape[dim] - width, None, axis=dim)
    head = lax.slice_in_dim(block, 0, width, axis=dim)
    if lax.axis_size(axis) == 2:
        both = from_behind(jnp.concatenate([tail, head], axis=dim), axis, 1)
        low = lax.slice_in_dim(both, 0, width, axis=dim)
        high = lax.slice_in_dim(both, width, None, axis=dim)
    else:
        low = from_behind(tail, axis, 1)
        high = from_behind(head, axis, -1)
    return jnp.concatenate([low, block, high], axis=dim)


def cyclic_decayed_sum(held, gain_of):
    count = held.shape[0]
    result, offset, span, block, left = None, 0, 1, held, count
    while left:
        if left & 1:
            term = jnp.roll(block, offset, axis=0)
            if offset:
                term = gain_of(offset) * term
            result = term if result is None else result + term
            offset += span
        left >>= 1
        if left:
            block = block + gain_of(span) * jnp.roll(block, span, axis=0)
            span *= 2
    return result


def entering_sums(outgoing, rate_full, layers):
    shape = outgoing.shape
    size = outgoing.size
    count = lax.axis_size("gz")
    me = lax.axis_index("gz")
    chunk = -(-size // (count * TILE)) * TILE
    padded = chunk * count

    def spread(values, fill):
        flat = jnp.pad(values.reshape(-1), (0, padded - size), constant_values=fill)
        return flat.reshape(count, TILE_ROWS, chunk // TILE_ROWS)

    held = lax.all_to_all(spread(outgoing, 0.0), "gz", 0, 0, tiled=True)
    held = held.reshape(count, chunk)
    my_rates = lax.dynamic_index_in_dim(spread(rate_full, 1.0).reshape(count, chunk), me, 0, False)
    sums = cyclic_decayed_sum(held, lambda steps: jnp.exp(-my_rates * (layers * steps)))
    sums = jnp.roll(sums, 1, axis=0) / (1.0 - jnp.exp(-my_rates * (layers * count)))
    sums = sums.reshape(count, TILE_ROWS, chunk // TILE_ROWS)
    back = lax.all_to_all(sums, "gz", 0, 0, tiled=True)
    return back.reshape(-1)[:size].reshape(shape)


def shift_kernel(steps_ref, terms_ref, entering_ref, before_ref, factor_ref, cos_ref, sin_ref,
                 real_ref, imag_ref, field_ref):
    _, layers, ext_columns, rows, width = terms_ref.shape
    _, columns, _, _ = real_ref.shape
    factor = factor_ref[...]
    starts = [jnp.clip(R - steps_ref[entry, 0], 0, 2 * R) for entry in range(NOFF)]
    turns = [lax.rem(steps_ref[entry, 1] + rows, rows) for entry in range(NOFF)]

    def build(c, carry):
        state = entering_ref[:, c]
        prev_term = before_ref[:, c].astype(jnp.float32)
        for i in range(layers):
            up = factor * (state - prev_term)
            fresh = terms_ref[:, i, c]
            state = factor * state + fresh
            prev_term = fresh
            field_ref[i, :, c] = up.astype(jnp.bfloat16).astype(jnp.float32)
        return carry

    lax.fori_loop(0, ext_columns, build, 0, unroll=4)
    for i in range(layers):

        def column(x, carry, i=i):
            acc_real = jnp.zeros((rows, width), jnp.float32)
            acc_imag = jnp.zeros((rows, width), jnp.float32)
            for entry in range(NOFF):
                moved = field_ref[i, :, starts[entry] + x, :, :]
                moved = pltpu.roll(moved, turns[entry], 1)
                cosine = cos_ref[entry]
                sine_part = sin_ref[entry]
                acc_real = acc_real + moved[0] * cosine - moved[1] * sine_part
                acc_imag = acc_imag + moved[0] * sine_part + moved[1] * cosine
            real_ref[i, x] = acc_real.astype(real_ref.dtype)
            imag_ref[i, x] = acc_imag.astype(imag_ref.dtype)
            return carry

        lax.fori_loop(0, columns, column, 0, unroll=4)


def shift_layers(offsets, box_terms, entering, before_term, rate, wave_x, wave_y, columns):
    _, layers, boxes, width = box_terms.shape
    factor = jnp.exp(-rate)[None, :]
    steps = offsets.astype(jnp.float32)
    phase_angle = steps[:, :1] * wave_x[None] + steps[:, 1:] * wave_y[None]
    vmem = pl.BlockSpec(memory_space=pltpu.VMEM)
    smem = pl.BlockSpec(memory_space=pltpu.SMEM)
    half = jax.ShapeDtypeStruct((layers, columns, BY, width), jnp.bfloat16)
    return pl.pallas_call(
        shift_kernel,
        out_shape=(half, half),
        in_specs=[smem] + [vmem] * 6,
        out_specs=(vmem, vmem),
        scratch_shapes=[pltpu.VMEM((layers, 2, boxes // BY, BY, width), jnp.float32)],
        cost_estimate=pl.CostEstimate(
            flops=2 * layers * boxes * width * 30,
            transcendentals=0,
            bytes_accessed=box_terms.size * 4 + 3 * entering.size * 4,
        ),
    )(offsets, box_terms.reshape(2, layers, boxes // BY, BY, width),
      entering.reshape(2, boxes // BY, BY, width), before_term.reshape(2, boxes // BY, BY, width), factor,
      jnp.broadcast_to(jnp.cos(phase_angle)[:, None, :], (NOFF, BY, width)),
      jnp.broadcast_to(jnp.sin(phase_angle)[:, None, :], (NOFF, BY, width)))


def body(moments, counts, m2x, x2l, decay_rate, wave_x, wave_y, offsets):
    coeffs, layers, plane_size = moments.shape
    exp_rows = m2x.shape[0]
    half_rows = exp_rows // 2
    columns = plane_size // BY
    ext_columns = columns + 2 * R
    ext_boxes = ext_columns * BY
    rate = decay_rate[None, None, None, :]
    factor = jnp.exp(-rate)
    weight = jnp.sqrt(1.0 - factor * factor)
    multipole = (moments.astype(jnp.float32) * counts.astype(jnp.float32)[None]).astype(
        jnp.bfloat16
    )
    multipole = with_halo(multipole, "xy", 2, R * BY).reshape(coeffs, layers * ext_boxes)
    halves = []
    for part in range(2):
        rows = m2x[part * half_rows : (part + 1) * half_rows]
        expansion = lax.dot_general(
            multipole, rows, (((0,), (1,)), ((), ())), preferred_element_type=jnp.float32
        )
        halves.append(expansion.reshape(layers, ext_boxes, half_rows))
    box_terms = weight * jnp.stack(halves)

    outgoing = box_terms[:, layers - 1]
    for j in range(layers - 1):
        outgoing = outgoing + jnp.exp(-rate[0] * float(layers - 1 - j)) * box_terms[:, j]
    outgoing, box_terms = lax.optimization_barrier((outgoing, box_terms))
    before_term = from_behind(box_terms[:, layers - 1].astype(jnp.bfloat16), "gz", 1)

    rate_full = jnp.broadcast_to(decay_rate, outgoing.shape)
    entering = entering_sums(outgoing, rate_full, float(layers))

    shifted = shift_layers(
        offsets, box_terms, entering, before_term, decay_rate, wave_x, wave_y, columns
    )
    local_out = None
    for part in range(2):
        product = lax.dot_general(
            x2l[:, part * half_rows : (part + 1) * half_rows],
            shifted[part].reshape(layers * plane_size, half_rows),
            (((1,), (1,)), ((), ())),
            preferred_element_type=jnp.float32,
        )
        local_out = product if local_out is None else local_out + product
    return local_out.astype(jnp.bfloat16).reshape(coeffs, layers, plane_size)


def solution(mesh):
    in_specs = (P(None, "gz", "xy"), P("gz", "xy"), P(), P(), P(), P(), P(), P())
    out_specs = P(None, "gz", "xy")
    return jax.shard_map(body, mesh=mesh, in_specs=in_specs, out_specs=out_specs, check_vma=False)
```

```python
import jax
import jax.numpy as jnp
from jax import lax
from jax.experimental import pallas as pl
from jax.experimental.pallas import tpu as pltpu
from jax.sharding import PartitionSpec as P

BY = 8
R = 2
NOFF = 6
TILE_ROWS = 8
TILE = TILE_ROWS * 512


def from_behind(value, axis, steps):
    count = lax.axis_size(axis)
    pairs = [(source, (source + steps) % count) for source in range(count)]
    return lax.ppermute(value, axis, pairs)


def with_halo(block, axis, dim, width):
    tail = lax.slice_in_dim(block, block.shape[dim] - width, None, axis=dim)
    head = lax.slice_in_dim(block, 0, width, axis=dim)
    if lax.axis_size(axis) == 2:
        both = from_behind(jnp.concatenate([tail, head], axis=dim), axis, 1)
        low = lax.slice_in_dim(both, 0, width, axis=dim)
        high = lax.slice_in_dim(both, width, None, axis=dim)
    else:
        low = from_behind(tail, axis, 1)
        high = from_behind(head, axis, -1)
    return jnp.concatenate([low, block, high], axis=dim)


def cyclic_decayed_sum(held, gain_of):
    count = held.shape[0]
    result, offset, span, block, left = None, 0, 1, held, count
    while left:
        if left & 1:
            term = jnp.roll(block, offset, axis=0)
            if offset:
                term = gain_of(offset) * term
            result = term if result is None else result + term
            offset += span
        left >>= 1
        if left:
            block = block + gain_of(span) * jnp.roll(block, span, axis=0)
            span *= 2
    return result


def entering_sums(outgoing, rate_full, layers):
    shape = outgoing.shape
    size = outgoing.size
    count = lax.axis_size("gz")
    me = lax.axis_index("gz")
    chunk = -(-size // (count * TILE)) * TILE
    padded = chunk * count

    def spread(values, fill):
        flat = jnp.pad(values.reshape(-1), (0, padded - size), constant_values=fill)
        return flat.reshape(count, TILE_ROWS, chunk // TILE_ROWS)

    held = lax.all_to_all(spread(outgoing, 0.0), "gz", 0, 0, tiled=True)
    held = held.reshape(count, chunk)
    my_rates = lax.dynamic_index_in_dim(spread(rate_full, 1.0).reshape(count, chunk), me, 0, False)
    sums = cyclic_decayed_sum(held, lambda steps: jnp.exp(-my_rates * (layers * steps)))
    sums = jnp.roll(sums, 1, axis=0) / (1.0 - jnp.exp(-my_rates * (layers * count)))
    sums = sums.reshape(count, TILE_ROWS, chunk // TILE_ROWS)
    back = lax.all_to_all(sums, "gz", 0, 0, tiled=True)
    return back.reshape(-1)[:size].reshape(shape)


def shift_kernel(steps_ref, terms_ref, entering_ref, before_ref, factor_ref, cos_ref, sin_ref,
                 real_ref, imag_ref, field_ref):
    _, layers, ext_columns, rows, width = terms_ref.shape
    _, columns, _, _ = real_ref.shape
    factor = factor_ref[...]
    starts = [jnp.clip(R - steps_ref[entry, 0], 0, 2 * R) for entry in range(NOFF)]
    turns = [lax.rem(steps_ref[entry, 1] + rows, rows) for entry in range(NOFF)]

    def build(c, carry):
        state = entering_ref[:, c]
        prev_term = before_ref[:, c].astype(jnp.float32)
        for i in range(layers):
            up = factor * (state - prev_term)
            fresh = terms_ref[:, i, c]
            state = factor * state + fresh
            prev_term = fresh
            field_ref[i, :, c] = up.astype(jnp.bfloat16).astype(jnp.float32)
        return carry

    lax.fori_loop(0, ext_columns, build, 0)
    for i in range(layers):

        def column(x, carry, i=i):
            acc_real = jnp.zeros((rows, width), jnp.float32)
            acc_imag = jnp.zeros((rows, width), jnp.float32)
            for entry in range(NOFF):
                moved = field_ref[i, :, starts[entry] + x, :, :]
                moved = pltpu.roll(moved, turns[entry], 1)
                cosine = cos_ref[entry]
                sine_part = sin_ref[entry]
                acc_real = acc_real + moved[0] * cosine - moved[1] * sine_part
                acc_imag = acc_imag + moved[0] * sine_part + moved[1] * cosine
            real_ref[i, x] = acc_real.astype(real_ref.dtype)
            imag_ref[i, x] = acc_imag.astype(imag_ref.dtype)
            return carry

        lax.fori_loop(0, columns, column, 0, unroll=16)


def shift_layers(offsets, box_terms, entering, before_term, rate, wave_x, wave_y, columns):
    _, layers, boxes, width = box_terms.shape
    factor = jnp.exp(-rate)[None, :]
    steps = offsets.astype(jnp.float32)
    phase_angle = steps[:, :1] * wave_x[None] + steps[:, 1:] * wave_y[None]
    vmem = pl.BlockSpec(memory_space=pltpu.VMEM)
    smem = pl.BlockSpec(memory_space=pltpu.SMEM)
    half = jax.ShapeDtypeStruct((layers, columns, BY, width), jnp.bfloat16)
    return pl.pallas_call(
        shift_kernel,
        out_shape=(half, half),
        in_specs=[smem] + [vmem] * 6,
        out_specs=(vmem, vmem),
        scratch_shapes=[pltpu.VMEM((layers, 2, boxes // BY, BY, width), jnp.float32)],
        cost_estimate=pl.CostEstimate(
            flops=2 * layers * boxes * width * 30,
            transcendentals=0,
            bytes_accessed=box_terms.size * 4 + 3 * entering.size * 4,
        ),
    )(offsets, box_terms.reshape(2, layers, boxes // BY, BY, width),
      entering.reshape(2, boxes // BY, BY, width), before_term.reshape(2, boxes // BY, BY, width), factor,
      jnp.broadcast_to(jnp.cos(phase_angle)[:, None, :], (NOFF, BY, width)),
      jnp.broadcast_to(jnp.sin(phase_angle)[:, None, :], (NOFF, BY, width)))


def body(moments, counts, m2x, x2l, decay_rate, wave_x, wave_y, offsets):
    coeffs, layers, plane_size = moments.shape
    exp_rows = m2x.shape[0]
    half_rows = exp_rows // 2
    columns = plane_size // BY
    ext_columns = columns + 2 * R
    ext_boxes = ext_columns * BY
    rate = decay_rate[None, None, None, :]
    factor = jnp.exp(-rate)
    weight = jnp.sqrt(1.0 - factor * factor)
    multipole = (moments.astype(jnp.float32) * counts.astype(jnp.float32)[None]).astype(
        jnp.bfloat16
    )
    multipole = with_halo(multipole, "xy", 2, R * BY).reshape(coeffs, layers * ext_boxes)
    halves = []
    for part in range(2):
        rows = m2x[part * half_rows : (part + 1) * half_rows]
        expansion = lax.dot_general(
            multipole, rows, (((0,), (1,)), ((), ())), preferred_element_type=jnp.float32
        )
        halves.append(expansion.reshape(layers, ext_boxes, half_rows))
    box_terms = weight * jnp.stack(halves)

    outgoing = box_terms[:, layers - 1]
    for j in range(layers - 1):
        outgoing = outgoing + jnp.exp(-rate[0] * float(layers - 1 - j)) * box_terms[:, j]
    outgoing, box_terms = lax.optimization_barrier((outgoing, box_terms))
    before_term = from_behind(box_terms[:, layers - 1].astype(jnp.bfloat16), "gz", 1)

    rate_full = jnp.broadcast_to(decay_rate, outgoing.shape)
    entering = entering_sums(outgoing, rate_full, float(layers))

    shifted = shift_layers(
        offsets, box_terms, entering, before_term, decay_rate, wave_x, wave_y, columns
    )
    local_out = None
    for part in range(2):
        product = lax.dot_general(
            x2l[:, part * half_rows : (part + 1) * half_rows],
            shifted[part].reshape(layers * plane_size, half_rows),
            (((1,), (1,)), ((), ())),
            preferred_element_type=jnp.float32,
        )
        local_out = product if local_out is None else local_out + product
    return local_out.astype(jnp.bfloat16).reshape(coeffs, layers, plane_size)


def solution(mesh):
    in_specs = (P(None, "gz", "xy"), P("gz", "xy"), P(), P(), P(), P(), P(), P())
    out_specs = P(None, "gz", "xy")
    return jax.shard_map(body, mesh=mesh, in_specs=in_specs, out_specs=out_specs, check_vma=False)
```

```python
import jax
import jax.numpy as jnp
from jax import lax
from jax.experimental import pallas as pl
from jax.experimental.pallas import tpu as pltpu
from jax.sharding import PartitionSpec as P

BY = 8
R = 2
NOFF = 6
TILE_ROWS = 8
TILE = TILE_ROWS * 512


def from_behind(value, axis, steps):
    count = lax.axis_size(axis)
    pairs = [(source, (source + steps) % count) for source in range(count)]
    return lax.ppermute(value, axis, pairs)


def with_halo(block, axis, dim, width):
    tail = lax.slice_in_dim(block, block.shape[dim] - width, None, axis=dim)
    head = lax.slice_in_dim(block, 0, width, axis=dim)
    if lax.axis_size(axis) == 2:
        both = from_behind(jnp.concatenate([tail, head], axis=dim), axis, 1)
        low = lax.slice_in_dim(both, 0, width, axis=dim)
        high = lax.slice_in_dim(both, width, None, axis=dim)
    else:
        low = from_behind(tail, axis, 1)
        high = from_behind(head, axis, -1)
    return jnp.concatenate([low, block, high], axis=dim)


def cyclic_decayed_sum(held, gain_of):
    count = held.shape[0]
    result, offset, span, block, left = None, 0, 1, held, count
    while left:
        if left & 1:
            term = jnp.roll(block, offset, axis=0)
            if offset:
                term = gain_of(offset) * term
            result = term if result is None else result + term
            offset += span
        left >>= 1
        if left:
            block = block + gain_of(span) * jnp.roll(block, span, axis=0)
            span *= 2
    return result


def entering_sums(outgoing, rate_full, layers):
    shape = outgoing.shape
    size = outgoing.size
    count = lax.axis_size("gz")
    me = lax.axis_index("gz")
    chunk = -(-size // (count * TILE)) * TILE
    padded = chunk * count

    def spread(values, fill):
        flat = jnp.pad(values.reshape(-1), (0, padded - size), constant_values=fill)
        return flat.reshape(count, TILE_ROWS, chunk // TILE_ROWS)

    held = lax.all_to_all(spread(outgoing, 0.0), "gz", 0, 0, tiled=True)
    held = held.reshape(count, chunk)
    my_rates = lax.dynamic_index_in_dim(spread(rate_full, 1.0).reshape(count, chunk), me, 0, False)
    sums = cyclic_decayed_sum(held, lambda steps: jnp.exp(-my_rates * (layers * steps)))
    sums = jnp.roll(sums, 1, axis=0) / (1.0 - jnp.exp(-my_rates * (layers * count)))
    sums = sums.reshape(count, TILE_ROWS, chunk // TILE_ROWS)
    back = lax.all_to_all(sums, "gz", 0, 0, tiled=True)
    return back.reshape(-1)[:size].reshape(shape)


def shift_kernel(steps_ref, terms_ref, entering_ref, before_ref, factor_ref, cos_ref, sin_ref,
                 real_ref, imag_ref, field_ref):
    _, layers, ext_columns, rows, width = terms_ref.shape
    _, columns, _, _ = real_ref.shape
    factor = factor_ref[...]
    starts = [jnp.clip(R - steps_ref[entry, 0], 0, 2 * R) for entry in range(NOFF)]
    turns = [lax.rem(steps_ref[entry, 1] + rows, rows) for entry in range(NOFF)]

    def build(c, carry):
        state = entering_ref[:, c]
        prev_term = before_ref[:, c].astype(jnp.float32)
        for i in range(layers):
            up = factor * (state - prev_term)
            fresh = terms_ref[:, i, c]
            state = factor * state + fresh
            prev_term = fresh
            field_ref[i, :, c] = up.astype(jnp.bfloat16).astype(jnp.float32)
        return carry

    lax.fori_loop(0, ext_columns, build, 0)
    for i in range(layers):

        def column(x, carry, i=i):
            acc_real = jnp.zeros((rows, width), jnp.float32)
            acc_imag = jnp.zeros((rows, width), jnp.float32)
            for entry in range(NOFF):
                moved = field_ref[i, :, starts[entry] + x, :, :]
                moved = pltpu.roll(moved, turns[entry], 1)
                cosine = cos_ref[entry]
                sine_part = sin_ref[entry]
                acc_real = acc_real + moved[0] * cosine - moved[1] * sine_part
                acc_imag = acc_imag + moved[0] * sine_part + moved[1] * cosine
            real_ref[i, x] = acc_real.astype(real_ref.dtype)
            imag_ref[i, x] = acc_imag.astype(imag_ref.dtype)
            return carry

        lax.fori_loop(0, columns, column, 0, unroll=4)


def shift_layers(offsets, box_terms, entering, before_term, rate, wave_x, wave_y, columns):
    _, layers, boxes, width = box_terms.shape
    factor = jnp.exp(-rate)[None, :]
    steps = offsets.astype(jnp.float32)
    phase_angle = steps[:, :1] * wave_x[None] + steps[:, 1:] * wave_y[None]
    vmem = pl.BlockSpec(memory_space=pltpu.VMEM)
    smem = pl.BlockSpec(memory_space=pltpu.SMEM)
    half = jax.ShapeDtypeStruct((layers, columns, BY, width), jnp.bfloat16)
    return pl.pallas_call(
        shift_kernel,
        out_shape=(half, half),
        in_specs=[smem] + [vmem] * 6,
        out_specs=(vmem, vmem),
        scratch_shapes=[pltpu.VMEM((layers, 2, boxes // BY, BY, width), jnp.float32)],
        cost_estimate=pl.CostEstimate(
            flops=2 * layers * boxes * width * 30,
            transcendentals=0,
            bytes_accessed=box_terms.size * 4 + 3 * entering.size * 4,
        ),
    )(offsets, box_terms.reshape(2, layers, boxes // BY, BY, width),
      entering.reshape(2, boxes // BY, BY, width), before_term.reshape(2, boxes // BY, BY, width), factor,
      jnp.broadcast_to(jnp.cos(phase_angle)[:, None, :], (NOFF, BY, width)),
      jnp.broadcast_to(jnp.sin(phase_angle)[:, None, :], (NOFF, BY, width)))


def body(moments, counts, m2x, x2l, decay_rate, wave_x, wave_y, offsets):
    coeffs, layers, plane_size = moments.shape
    exp_rows = m2x.shape[0]
    half_rows = exp_rows // 2
    columns = plane_size // BY
    ext_columns = columns + 2 * R
    ext_boxes = ext_columns * BY
    rate = decay_rate[None, None, None, :]
    factor = jnp.exp(-rate)
    weight = jnp.sqrt(1.0 - factor * factor)
    multipole = (moments.astype(jnp.float32) * counts.astype(jnp.float32)[None]).astype(
        jnp.bfloat16
    )
    multipole = with_halo(multipole, "xy", 2, R * BY).reshape(coeffs, layers * ext_boxes)
    halves = []
    for part in range(2):
        rows = m2x[part * half_rows : (part + 1) * half_rows]
        expansion = lax.dot_general(
            multipole, rows, (((0,), (1,)), ((), ())), preferred_element_type=jnp.float32
        )
        halves.append(weight[0] * expansion.reshape(layers, ext_boxes, half_rows))
    box_terms = jnp.stack(halves)

    outgoing = box_terms[:, layers - 1]
    for j in range(layers - 1):
        outgoing = outgoing + jnp.exp(-rate[0] * float(layers - 1 - j)) * box_terms[:, j]
    outgoing, box_terms = lax.optimization_barrier((outgoing, box_terms))
    before_term = from_behind(box_terms[:, layers - 1].astype(jnp.bfloat16), "gz", 1)

    rate_full = jnp.broadcast_to(decay_rate, outgoing.shape)
    entering = entering_sums(outgoing, rate_full, float(layers))

    shifted = shift_layers(
        offsets, box_terms, entering, before_term, decay_rate, wave_x, wave_y, columns
    )
    local_out = None
    for part in range(2):
        product = lax.dot_general(
            x2l[:, part * half_rows : (part + 1) * half_rows],
            shifted[part].reshape(layers * plane_size, half_rows),
            (((1,), (1,)), ((), ())),
            preferred_element_type=jnp.float32,
        )
        local_out = product if local_out is None else local_out + product
    return local_out.astype(jnp.bfloat16).reshape(coeffs, layers, plane_size)


def solution(mesh):
    in_specs = (P(None, "gz", "xy"), P("gz", "xy"), P(), P(), P(), P(), P(), P())
    out_specs = P(None, "gz", "xy")
    return jax.shard_map(body, mesh=mesh, in_specs=in_specs, out_specs=out_specs, check_vma=False)
```
